128 devices in a mesh: dp: 8 (over y, z_lo), ctx: 16 (over z_hi, x, core).
Axes of the slice: x: 4, y: 4, z: 4 (z_hi: 2, z_lo: 2; z = z_hi * 2 + z_lo), core: 2. Of those that a mesh axis runs over, the one named last changes fastest.
Arguments:
- queries: bfloat16 [8, 12288, 2048], P('dp', 'ctx'), may hold values from -200 to 200
- keys: bfloat16 [8, 12288, 2048], P('dp', 'ctx'), may hold values from -6 to 6
- values: bfloat16 [8, 12288, 2048], P('dp', 'ctx'), may hold values from -6 to 6
- grad_out: bfloat16 [8, 12288, 2048], P('dp', 'ctx'), may hold values from -6 to 6
- out_weight: bfloat16 [2048, 2048], P('dp'), may hold values from -0.125 to 0.125
- pattern: int32 [8, 96, 2], P('dp', 'ctx'), may hold values from 0 to 95, as said below
Outputs:
- mixed: bfloat16 [8, 12288, 2048], P('dp', 'ctx')
- query_grad: bfloat16 [8, 12288, 2048], P('dp', 'ctx')
- weight_grad: float32 [2048, 2048], P('dp')
The draws below stay inside these ranges and needn't reach their ends.
Inputs may be any that keep to these rules, and one draw needn't show every extreme that they name: `pattern`: key block c of a trace holds positions 128 * c onward and lies on ctx device c // 6. For each trace, the 12 entries of the query blocks of one ctx device name key blocks on pairwise distinct ctx devices.
All inputs are finite; a program needn't handle non-finite values.
Results may differ from the reference program's by a relative error of at most 0.014.
Values may be sent and summed in bfloat16 or wider, within the bound.
No kernel may reach another device: no remote copies, remote signals or barrier semaphores. Data moves between devices by JAX's collectives and lax.ppermute only.
A program may use at most 192 MiB of HBM per device.

```python
import math
import jax
import jax.numpy as jnp
from jax import lax

HEADS = 16
DH = 128
DOUT = 2048
BLK = 128
KSEL = 2
HD = 2048
QBLK = 6
TRACES = 8
SEQ = 12288
NQB = 96


def pattern_table(key):
    base = jax.random.fold_in(key, 71)
    groups = NQB // QBLK
    streams = jax.random.split(jax.random.fold_in(base, 1), TRACES * groups)
    owners = jax.vmap(lambda stream: jax.random.permutation(stream, groups))(streams)
    owners = owners[:, :QBLK * KSEL]
    local = jax.random.randint(jax.random.fold_in(base, 2), (TRACES * groups, QBLK * KSEL), 0, QBLK)
    table = owners * QBLK + local
    return table.reshape(TRACES, NQB, KSEL).astype(jnp.int32)


def key_field(key):
    field = jax.random.normal(jax.random.fold_in(key, 72), (TRACES, SEQ, HD), jnp.float32)
    field = jnp.clip(field, -6.0, 6.0)
    return field


def draw_pattern(key, part):
    return pattern_table(key)


def draw_keys(key, part):
    return key_field(key).astype(jnp.bfloat16)


def draw_queries(key, part):
    field = jax.random.normal(jax.random.fold_in(key, 73), (TRACES, SEQ, HD), jnp.float32)
    field = jnp.clip(field, -6.0, 6.0)
    return field.astype(jnp.bfloat16)


def spiked(entries, stream_key, source, target, blocks, factor):
    def block_of(position):
        return (jnp.arange(entries.shape[position]) // (entries.shape[position] // blocks)).reshape((-1,) + (1,) * (entries.ndim - 1 - position))

    near = jax.random.permutation(stream_key, blocks)[block_of(target)]
    other_side = (block_of(target) + blocks // 2) % blocks
    return jnp.where((block_of(source) == near) | (block_of(source) == other_side), factor * entries, entries)


def block_levels(rng, dims, shards, low, high):
    factor_of, own = 1.0, jax.random.fold_in(rng, 6)
    for position, parts in shards:
        steps = jnp.exp(jax.random.uniform(jax.random.fold_in(own, position), (parts,), jnp.float32, low / len(shards), high / len(shards)))
        factor_of = factor_of * jnp.repeat(steps, dims[position] // parts).reshape([-1 if axis == position else 1 for axis in range(len(dims))])
    return factor_of


def centred(key, shape, deviation, bound, shards=(), held_as=jnp.bfloat16):
    entries = jax.random.normal(key, shape, jnp.float32) * deviation
    if len(shards) > 0:
        entries = block_levels(key, shape, shards, -0.22, 0.18) * entries
    return jnp.clip(entries, min=-bound, max=bound).astype(held_as)


def bell_draw_with(own_key, extent, deviation, bound, shards, heavy, kind=jnp.bfloat16):
    values = deviation * jax.random.normal(own_key, extent, jnp.float32)
    if shards:
        values = values * block_levels(own_key, extent, shards, -0.22, 0.18)
    return jnp.clip(spiked(values, jax.random.fold_in(own_key, 3), *heavy), -bound, bound).astype(kind)


def setup_inputs(seed: int = 0) -> dict:
    streams_of = jax.random.split(jax.random.key(seed), 7)
    queries = draw_queries(jax.random.fold_in(streams_of[6], 71), 0)
    keys = draw_keys(jax.random.fold_in(streams_of[6], 71), 0)
    values = bell_draw_with(streams_of[2], (TRACES, SEQ, HD), 1.0, 6.0, ((0, 8), (1, 16)), (1, 2, 16, 2.0))
    grad_out = centred(streams_of[3], (TRACES, SEQ, DOUT), 1.0, 6.0, ((0, 8), (1, 16)))
    out_weight = centred(streams_of[4], (HD, DOUT), HD ** -0.5, 0.125, ((0, 8),))
    pattern = draw_pattern(jax.random.fold_in(streams_of[6], 71), 0)
    return {"queries": queries, "keys": keys, "values": values, "grad_out": grad_out, "out_weight": out_weight, "pattern": pattern}


def select_blocks(field, flat_table):
    blocks = field.reshape(NQB, BLK, HEADS, DH)
    picked = jnp.take(blocks, flat_table, axis=0)
    return picked.reshape(NQB, KSEL * BLK, HEADS, DH).astype(jnp.float32)

def softmax_rows(scores):
    top = lax.optimization_barrier(jnp.max(scores, axis=-1, keepdims=True))
    weights = jnp.exp(scores - top)
    return weights / lax.optimization_barrier(jnp.sum(weights, axis=-1, keepdims=True))

def trace_probs(queries, keys, table):
    picked_keys = select_blocks(keys, table.reshape(-1))
    query_rows = queries.reshape(NQB, BLK, HEADS, DH).astype(jnp.float32)
    scores = jnp.einsum('qrhd,qkhd->qhrk', query_rows, picked_keys) * (1.0 / math.sqrt(DH))
    return (softmax_rows(scores), picked_keys)

def trace_forward(inputs):
    queries, keys, values, table = inputs
    probs, picked_keys = trace_probs(queries, keys, table)
    picked_values = select_blocks(values, table.reshape(-1))
    weights = probs.astype(jnp.bfloat16).astype(jnp.float32)
    attention = jnp.einsum('qhrk,qkhd->qrhd', weights, picked_values)
    return attention.astype(jnp.bfloat16).reshape(SEQ, HD)

def trace_backward(inputs):
    queries, keys, values, table, attention, back = inputs
    probs, picked_keys = trace_probs(queries, keys, table)
    picked_values = select_blocks(values, table.reshape(-1))
    back_rows = back.reshape(NQB, BLK, HEADS, DH).astype(jnp.float32)
    attention_rows = attention.reshape(NQB, BLK, HEADS, DH).astype(jnp.float32)
    dprobs = jnp.einsum('qrhd,qkhd->qhrk', back_rows, picked_values)
    delta = jnp.einsum('qrhd,qrhd->qhr', back_rows, attention_rows)[..., None]
    dscores = (probs * (dprobs - delta)).astype(jnp.bfloat16).astype(jnp.float32)
    result = jnp.einsum('qhrk,qkhd->qrhd', dscores, picked_keys) * (1.0 / math.sqrt(DH))
    return result.astype(jnp.bfloat16).reshape(SEQ, HD)

def reference(queries, keys, values, grad_out, out_weight, pattern):
    attention = lax.map(trace_forward, (queries, keys, values, pattern))
    flat_attention = attention.reshape(TRACES * SEQ, HD)
    flat_grad = grad_out.reshape(TRACES * SEQ, DOUT)
    mixed = jnp.dot(flat_attention, out_weight, preferred_element_type=jnp.float32)
    mixed = mixed.astype(jnp.bfloat16).reshape(TRACES, SEQ, DOUT)
    back = jnp.dot(flat_grad, out_weight.T, preferred_element_type=jnp.float32)
    back = back.astype(jnp.bfloat16).reshape(TRACES, SEQ, HD)
    weight_grad = jnp.dot(flat_attention.T, flat_grad, preferred_element_type=jnp.float32)
    weight_grad = weight_grad / math.sqrt(TRACES * SEQ)
    query_grad = lax.map(trace_backward, (queries, keys, values, pattern, attention, back))
    return (mixed, query_grad, weight_grad)
```

```python
import math

import jax
import jax.numpy as jnp
from jax import lax
from jax.sharding import PartitionSpec as P

HEADS = 16
DH = 128
BLK = 128
KSEL = 2


def softmax_rows(scores):
    top = jnp.max(scores, axis=-1, keepdims=True)
    weights = jnp.exp(scores - top)
    return weights / jnp.sum(weights, axis=-1, keepdims=True)


def local(queries, keys, values, grad_out, out_weight, pattern):
    ctx_count = lax.axis_size("ctx")
    data_count = lax.axis_size("dp")
    own_index = lax.axis_index("ctx")
    rows = queries.shape[1]
    blocks = rows // BLK
    width = HEADS * DH
    scale = 1.0 / math.sqrt(DH)
    query_rows = queries[0].reshape(blocks, BLK, HEADS, DH)
    key_blocks = keys[0].reshape(blocks, BLK, width)
    value_blocks = values[0].reshape(blocks, BLK, width)
    table = pattern[0]
    owner = table // blocks
    every_table = lax.all_gather(table, "ctx", axis=0, tiled=True).reshape(ctx_count, blocks * KSEL)
    wanted = every_table // blocks == own_index
    send_index = jnp.sum(jnp.where(wanted, every_table % blocks, 0), axis=1)
    send_flag = jnp.any(wanted, axis=1)
    flag = send_flag[:, None, None]
    empty = jnp.zeros((), jnp.bfloat16)
    send_keys = jnp.where(flag, jnp.take(key_blocks, send_index, axis=0), empty)
    send_values = jnp.where(flag, jnp.take(value_blocks, send_index, axis=0), empty)
    got_keys, got_values = (
        lax.all_to_all(send_keys, "ctx", split_axis=0, concat_axis=0, tiled=True),
        lax.all_to_all(send_values, "ctx", split_axis=0, concat_axis=0, tiled=True),
    )
    order = owner.reshape(-1)
    picked_keys = jnp.take(got_keys, order, axis=0).reshape(blocks, KSEL * BLK, HEADS, DH)
    picked_values = jnp.take(got_values, order, axis=0).reshape(blocks, KSEL * BLK, HEADS, DH)
    scores = (
        jnp.einsum("qrhd,qkhd->qhrk", query_rows, picked_keys, preferred_element_type=jnp.float32)
        * scale
    )
    probs = softmax_rows(scores)
    attention = jnp.einsum(
        "qhrk,qkhd->qrhd",
        probs.astype(jnp.bfloat16),
        picked_values,
        preferred_element_type=jnp.float32,
    )
    attention = attention.astype(jnp.bfloat16)
    attention_flat = attention.reshape(rows, width)
    grad_flat = grad_out[0]
    piece = lax.all_gather(out_weight, "dp", axis=0, tiled=True)
    columns = attention_flat
    total = jnp.dot(columns, piece, preferred_element_type=jnp.float32)
    part_back = lax.dot_general(
        grad_flat, piece, (((1,), (1,)), ((), ())), preferred_element_type=jnp.float32
    )
    back_sum = part_back
    mixed_sum, back_sum = (total, back_sum)
    mixed = mixed_sum.astype(jnp.bfloat16)
    back = back_sum.astype(jnp.bfloat16)
    split = width // (ctx_count * data_count)
    columns = (
        attention_flat.reshape(rows, data_count, ctx_count, split)
        .transpose(0, 2, 1, 3)
        .reshape(rows, width)
    )
    partial = lax.dot_general(
        columns, grad_flat, (((0,), (0,)), ((), ())), preferred_element_type=jnp.float32
    )
    stage = lax.psum_scatter(partial, "ctx", scatter_dimension=0, tiled=True)
    shard = lax.psum_scatter(stage, "dp", scatter_dimension=0, tiled=True)
    weight_sum = lax.all_gather(shard, "ctx", axis=0, tiled=True)
    weight_grad = weight_sum / math.sqrt(rows * ctx_count * data_count)
    back_rows = back.reshape(blocks, BLK, HEADS, DH)
    dprobs = jnp.einsum(
        "qrhd,qkhd->qhrk", back_rows, picked_values, preferred_element_type=jnp.float32
    )
    delta = jnp.einsum("qrhd,qrhd->qhr", back_rows, attention, preferred_element_type=jnp.float32)[
        ..., None
    ]
    dscores = (probs * (dprobs - delta)).astype(jnp.bfloat16)
    query_sum = (
        jnp.einsum("qhrk,qkhd->qrhd", dscores, picked_keys, preferred_element_type=jnp.float32)
        * scale
    )
    query_grad = query_sum.astype(jnp.bfloat16).reshape(rows, width)
    return (mixed[None], query_grad[None], weight_grad)


def solution(mesh):
    return jax.shard_map(
        local,
        mesh=mesh,
        in_specs=(
            P("dp", "ctx", None),
            P("dp", "ctx", None),
            P("dp", "ctx", None),
            P("dp", "ctx", None),
            P("dp", None),
            P("dp", "ctx", None),
        ),
        out_specs=(P("dp", "ctx", None), P("dp", "ctx", None), P("dp", None)),
        check_vma=False,
    )
```

```python
import math

import jax
import jax.numpy as jnp
from jax import lax
from jax.sharding import PartitionSpec as P

HEADS = 16
DH = 128
BLK = 128
KSEL = 2


def softmax_rows(scores):
    top = jnp.max(scores, axis=-1, keepdims=True)
    weights = jnp.exp(scores - top)
    return weights / jnp.sum(weights, axis=-1, keepdims=True)


def local(queries, keys, values, grad_out, out_weight, pattern):
    ctx_count = lax.axis_size("ctx")
    data_count = lax.axis_size("dp")
    own_index = lax.axis_index("ctx")
    rows = queries.shape[1]
    blocks = rows // BLK
    width = HEADS * DH
    scale = 1.0 / math.sqrt(DH)
    query_rows = queries[0].reshape(blocks, BLK, HEADS, DH)
    key_blocks = keys[0].reshape(blocks, BLK, width)
    value_blocks = values[0].reshape(blocks, BLK, width)
    table = pattern[0]
    owner = table // blocks
    every_table = lax.all_gather(table, "ctx", axis=0, tiled=True).reshape(ctx_count, blocks * KSEL)
    wanted = every_table // blocks == own_index
    send_index = jnp.sum(jnp.where(wanted, every_table % blocks, 0), axis=1)
    send_flag = jnp.any(wanted, axis=1)
    flag = send_flag[:, None, None]
    empty = jnp.zeros((), jnp.bfloat16)
    send_keys = jnp.where(flag, jnp.take(key_blocks, send_index, axis=0), empty)
    send_values = jnp.where(flag, jnp.take(value_blocks, send_index, axis=0), empty)
    got = lax.all_to_all(
        jnp.concatenate([send_keys, send_values], axis=-1), "ctx", split_axis=0, concat_axis=0, tiled=True
    )
    got_keys, got_values = got[..., :width], got[..., width:]
    order = owner.reshape(-1)
    picked_keys = jnp.take(got_keys, order, axis=0).reshape(blocks, KSEL * BLK, HEADS, DH)
    picked_values = jnp.take(got_values, order, axis=0).reshape(blocks, KSEL * BLK, HEADS, DH)
    scores = (
        jnp.einsum("qrhd,qkhd->qhrk", query_rows, picked_keys, preferred_element_type=jnp.float32)
        * scale
    )
    probs = softmax_rows(scores)
    attention = jnp.einsum(
        "qhrk,qkhd->qrhd",
        probs.astype(jnp.bfloat16),
        picked_values,
        preferred_element_type=jnp.float32,
    )
    attention = attention.astype(jnp.bfloat16)
    attention_flat = attention.reshape(rows, width)
    grad_flat = grad_out[0]
    half = out_weight.shape[1] // 2
    side = own_index % 2
    mine = lax.all_gather(
        lax.dynamic_slice_in_dim(out_weight, side * half, half, axis=1), "dp", axis=0, tiled=True
    )
    other = lax.ppermute(mine, "ctx", [(j, j ^ 1) for j in range(ctx_count)])
    first = jnp.where(side == 0, mine, other)
    second = jnp.where(side == 0, other, mine)
    mixed_sum = jnp.concatenate(
        [
            jnp.dot(attention_flat, first, preferred_element_type=jnp.float32),
            jnp.dot(attention_flat, second, preferred_element_type=jnp.float32),
        ],
        axis=1,
    )
    dims = (((1,), (1,)), ((), ()))
    back_sum = lax.dot_general(
        grad_flat[:, :half], first, dims, preferred_element_type=jnp.float32
    ) + lax.dot_general(grad_flat[:, half:], second, dims, preferred_element_type=jnp.float32)
    mixed = mixed_sum.astype(jnp.bfloat16)
    back = back_sum.astype(jnp.bfloat16)
    split = width // (ctx_count * data_count)
    columns = (
        attention_flat.reshape(rows, data_count, ctx_count, split)
        .transpose(0, 2, 1, 3)
        .reshape(rows, width)
    )
    partial = lax.dot_general(
        columns, grad_flat, (((0,), (0,)), ((), ())), preferred_element_type=jnp.float32
    )
    stage = lax.psum_scatter(partial.astype(jnp.bfloat16), "ctx", scatter_dimension=0, tiled=True)
    shard = lax.psum_scatter(stage.astype(jnp.float32), "dp", scatter_dimension=0, tiled=True)
    weight_sum = lax.all_gather(shard.astype(jnp.bfloat16), "ctx", axis=0, tiled=True).astype(
        jnp.float32
    )
    weight_grad = weight_sum / math.sqrt(rows * ctx_count * data_count)
    back_rows = back.reshape(blocks, BLK, HEADS, DH)
    dprobs = jnp.einsum(
        "qrhd,qkhd->qhrk", back_rows, picked_values, preferred_element_type=jnp.float32
    )
    delta = jnp.einsum("qrhd,qrhd->qhr", back_rows, attention, preferred_element_type=jnp.float32)[
        ..., None
    ]
    dscores = (probs * (dprobs - delta)).astype(jnp.bfloat16)
    query_sum = (
        jnp.einsum("qhrk,qkhd->qrhd", dscores, picked_keys, preferred_element_type=jnp.float32)
        * scale
    )
    query_grad = query_sum.astype(jnp.bfloat16).reshape(rows, width)
    return (mixed[None], query_grad[None], weight_grad)


def solution(mesh):
    return jax.shard_map(
        local,
        mesh=mesh,
        in_specs=(
            P("dp", "ctx", None),
            P("dp", "ctx", None),
            P("dp", "ctx", None),
            P("dp", "ctx", None),
            P("dp", None),
            P("dp", "ctx", None),
        ),
        out_specs=(P("dp", "ctx", None), P("dp", "ctx", None), P("dp", None)),
        check_vma=False,
    )
```

```python
import math

import jax
import jax.numpy as jnp
from jax import lax
from jax.sharding import PartitionSpec as P

HEADS = 16
DH = 128
BLK = 128
KSEL = 2


def softmax_rows(scores):
    top = jnp.max(scores, axis=-1, keepdims=True)
    weights = jnp.exp(scores - top)
    return weights / jnp.sum(weights, axis=-1, keepdims=True)


def local(queries, keys, values, grad_out, out_weight, pattern):
    ctx_count = lax.axis_size("ctx")
    data_count = lax.axis_size("dp")
    own_index = lax.axis_index("ctx")
    rows = queries.shape[1]
    blocks = rows // BLK
    width = HEADS * DH
    scale = 1.0 / math.sqrt(DH)
    query_rows = queries[0].reshape(blocks, BLK, HEADS, DH)
    key_blocks = keys[0].reshape(blocks, BLK, width)
    value_blocks = values[0].reshape(blocks, BLK, width)
    table = pattern[0]
    owner = table // blocks
    every_table = lax.all_gather(table, "ctx", axis=0, tiled=True).reshape(ctx_count, blocks * KSEL)
    wanted = every_table // blocks == own_index
    send_index = jnp.sum(jnp.where(wanted, every_table % blocks, 0), axis=1)
    got = lax.all_to_all(
        jnp.concatenate(
            [jnp.take(key_blocks, send_index, axis=0), jnp.take(value_blocks, send_index, axis=0)],
            axis=-1,
        ),
        "ctx",
        split_axis=0,
        concat_axis=0,
        tiled=True,
    )
    got_keys, got_values = got[..., :width], got[..., width:]
    order = owner.reshape(-1)
    picked_keys = jnp.take(got_keys, order, axis=0).reshape(blocks, KSEL * BLK, HEADS, DH)
    picked_values = jnp.take(got_values, order, axis=0).reshape(blocks, KSEL * BLK, HEADS, DH)
    scores = (
        jnp.einsum("qrhd,qkhd->qhrk", query_rows, picked_keys, preferred_element_type=jnp.float32)
        * scale
    )
    probs = softmax_rows(scores)
    attention = jnp.einsum(
        "qhrk,qkhd->qrhd",
        probs.astype(jnp.bfloat16),
        picked_values,
        preferred_element_type=jnp.float32,
    )
    attention = attention.astype(jnp.bfloat16)
    attention_flat = attention.reshape(rows, width)
    grad_flat = grad_out[0]
    half = out_weight.shape[1] // 2
    side = own_index % 2
    own_half = lax.dynamic_slice_in_dim(out_weight, side * half, half, axis=1)
    own_half, attention_flat = lax.optimization_barrier((own_half, attention_flat))
    mine = lax.all_to_all(
        jnp.broadcast_to(own_half[None], (data_count,) + own_half.shape),
        "dp",
        split_axis=0,
        concat_axis=0,
        tiled=True,
    ).reshape(data_count * own_half.shape[0], half)
    other = lax.ppermute(mine, "ctx", [(j, j ^ 1) for j in range(ctx_count)])
    first = jnp.where(side == 0, mine, other)
    second = jnp.where(side == 0, other, mine)
    mixed_sum = jnp.concatenate(
        [
            jnp.dot(attention_flat, first, preferred_element_type=jnp.float32),
            jnp.dot(attention_flat, second, preferred_element_type=jnp.float32),
        ],
        axis=1,
    )
    dims = (((1,), (1,)), ((), ()))
    back_sum = lax.dot_general(
        grad_flat[:, :half], first, dims, preferred_element_type=jnp.float32
    ) + lax.dot_general(grad_flat[:, half:], second, dims, preferred_element_type=jnp.float32)
    mixed = mixed_sum.astype(jnp.bfloat16)
    back = back_sum.astype(jnp.bfloat16)
    split = width // (ctx_count * data_count)
    columns = (
        attention_flat.reshape(rows, data_count, ctx_count, split)
        .transpose(0, 2, 1, 3)
        .reshape(rows, width)
    )
    partial = lax.dot_general(
        columns, grad_flat, (((0,), (0,)), ((), ())), preferred_element_type=jnp.float32
    )
    stage = lax.psum_scatter(partial.astype(jnp.bfloat16), "ctx", scatter_dimension=0, tiled=True)
    stage = stage.astype(jnp.float32) * (1.0 / math.sqrt(rows * ctx_count * data_count))
    shard = lax.psum_scatter(stage, "dp", scatter_dimension=0, tiled=True).reshape(split, width)
    weight_grad = lax.all_gather(shard.astype(jnp.bfloat16), "ctx", axis=0, tiled=True).astype(
        jnp.float32
    )
    back_rows = back.reshape(blocks, BLK, HEADS, DH)
    dprobs = jnp.einsum(
        "qrhd,qkhd->qhrk", back_rows, picked_values, preferred_element_type=jnp.float32
    )
    delta = jnp.einsum("qrhd,qrhd->qhr", back_rows, attention, preferred_element_type=jnp.float32)[
        ..., None
    ]
    dscores = (probs * (dprobs - delta)).astype(jnp.bfloat16)
    query_sum = (
        jnp.einsum("qhrk,qkhd->qrhd", dscores, picked_keys, preferred_element_type=jnp.float32)
        * scale
    )
    query_grad = query_sum.astype(jnp.bfloat16).reshape(rows, width)
    return (mixed[None], query_grad[None], weight_grad)


def solution(mesh):
    return jax.shard_map(
        local,
        mesh=mesh,
        in_specs=(
            P("dp", "ctx", None),
            P("dp", "ctx", None),
            P("dp", "ctx", None),
            P("dp", "ctx", None),
            P("dp", None),
            P("dp", "ctx", None),
        ),
        out_specs=(P("dp", "ctx", None), P("dp", "ctx", None), P("dp", None)),
        check_vma=False,
    )
```

```python
import math

import jax
import jax.numpy as jnp
from jax import lax
from jax.experimental import pallas as pl
from jax.experimental.pallas import tpu as pltpu
from jax.sharding import PartitionSpec as P

HEADS = 16
DH = 128
BLK = 128
KSEL = 2


def _fwd_kernel(table, q_ref, k0_ref, k1_ref, v0_ref, v1_ref, att_ref, probs_ref):
    scale = 1.0 / math.sqrt(DH)
    keys = jnp.concatenate([k0_ref[0], k1_ref[0]], axis=0)
    scores = lax.dot_general(
        q_ref[...], keys, (((1,), (1,)), ((), ())), preferred_element_type=jnp.float32
    ) * scale
    top = jnp.max(scores, axis=-1, keepdims=True)
    weights = jnp.exp(scores - top)
    probs = weights / jnp.sum(weights, axis=-1, keepdims=True)
    vals = jnp.concatenate([v0_ref[0], v1_ref[0]], axis=0)
    att = jnp.dot(probs.astype(jnp.bfloat16), vals, preferred_element_type=jnp.float32)
    att_ref[...] = att.astype(att_ref.dtype)
    probs_ref[0, 0] = probs

def forward_attention(query_flat, got, order, interpret=False):
    rows, width = query_flat.shape
    blocks = rows // BLK
    heads = width // DH
    def kv(k, off):
        return pl.BlockSpec((1, BLK, DH), lambda b, h, t: (t[KSEL * b + k], 0, off + h))
    grid_spec = pltpu.PrefetchScalarGridSpec(
        num_scalar_prefetch=1,
        grid=(blocks, heads),
        in_specs=[
            pl.BlockSpec((BLK, DH), lambda b, h, t: (b, h)),
            kv(0, 0), kv(1, 0), kv(0, heads), kv(1, heads),
        ],
        out_specs=[
            pl.BlockSpec((BLK, DH), lambda b, h, t: (b, h)),
            pl.BlockSpec((1, 1, BLK, KSEL * BLK), lambda b, h, t: (b, h, 0, 0)),
        ],
    )
    flops = blocks * heads * 4 * BLK * KSEL * BLK * DH
    return pl.pallas_call(
        _fwd_kernel,
        grid_spec=grid_spec,
        out_shape=[
            jax.ShapeDtypeStruct((rows, width), jnp.bfloat16),
            jax.ShapeDtypeStruct((blocks, heads, BLK, KSEL * BLK), jnp.float32),
        ],
        cost_estimate=pl.CostEstimate(
            flops=flops, transcendentals=blocks * heads * BLK * KSEL * BLK,
            bytes_accessed=rows * width * 2 * 3 + blocks * heads * BLK * KSEL * BLK * 4,
        ),
        interpret=interpret,
    )(order, query_flat, got, got, got, got)


def softmax_rows(scores):
    top = jnp.max(scores, axis=-1, keepdims=True)
    weights = jnp.exp(scores - top)
    return weights / jnp.sum(weights, axis=-1, keepdims=True)


def local(queries, keys, values, grad_out, out_weight, pattern):
    ctx_count = lax.axis_size("ctx")
    data_count = lax.axis_size("dp")
    own_index = lax.axis_index("ctx")
    rows = queries.shape[1]
    blocks = rows // BLK
    width = HEADS * DH
    scale = 1.0 / math.sqrt(DH)
    query_rows = queries[0].reshape(blocks, BLK, HEADS, DH)
    key_blocks = keys[0].reshape(blocks, BLK, width)
    value_blocks = values[0].reshape(blocks, BLK, width)
    table = pattern[0]
    owner = table // blocks
    every_table = lax.all_gather(table, "ctx", axis=0, tiled=True).reshape(ctx_count, blocks * KSEL)
    wanted = every_table // blocks == own_index
    send_index = jnp.sum(jnp.where(wanted, every_table % blocks, 0), axis=1)
    got = lax.all_to_all(
        jnp.concatenate(
            [jnp.take(key_blocks, send_index, axis=0), jnp.take(value_blocks, send_index, axis=0)],
            axis=-1,
        ),
        "ctx",
        split_axis=0,
        concat_axis=0,
        tiled=True,
    )
    got_keys, got_values = got[..., :width], got[..., width:]
    order = owner.reshape(-1)
    attention_flat, probs = forward_attention(queries[0], got, order)
    attention = attention_flat.reshape(blocks, BLK, HEADS, DH)
    picked_keys = jnp.take(got_keys, order, axis=0).reshape(blocks, KSEL * BLK, HEADS, DH)
    picked_values = jnp.take(got_values, order, axis=0).reshape(blocks, KSEL * BLK, HEADS, DH)
    grad_flat = grad_out[0]
    half = out_weight.shape[1] // 2
    side = own_index % 2
    own_half = lax.dynamic_slice_in_dim(out_weight, side * half, half, axis=1)
    own_half, attention_flat = lax.optimization_barrier((own_half, attention_flat))
    mine = lax.all_to_all(
        jnp.broadcast_to(own_half[None], (data_count,) + own_half.shape),
        "dp",
        split_axis=0,
        concat_axis=0,
        tiled=True,
    ).reshape(data_count * own_half.shape[0], half)
    other = lax.ppermute(mine, "ctx", [(j, j ^ 1) for j in range(ctx_count)])
    first = jnp.where(side == 0, mine, other)
    second = jnp.where(side == 0, other, mine)
    mixed_sum = jnp.concatenate(
        [
            jnp.dot(attention_flat, first, preferred_element_type=jnp.float32),
            jnp.dot(attention_flat, second, preferred_element_type=jnp.float32),
        ],
        axis=1,
    )
    dims = (((1,), (1,)), ((), ()))
    back_sum = lax.dot_general(
        grad_flat[:, :half], first, dims, preferred_element_type=jnp.float32
    ) + lax.dot_general(grad_flat[:, half:], second, dims, preferred_element_type=jnp.float32)
    mixed = mixed_sum.astype(jnp.bfloat16)
    back = back_sum.astype(jnp.bfloat16)
    split = width // (ctx_count * data_count)
    columns = (
        attention_flat.reshape(rows, data_count, ctx_count, split)
        .transpose(0, 2, 1, 3)
        .reshape(rows, width)
    )
    partial = lax.dot_general(
        columns, grad_flat, (((0,), (0,)), ((), ())), preferred_element_type=jnp.float32
    )
    stage = lax.psum_scatter(partial, "ctx", scatter_dimension=0, tiled=True)
    stage = stage * (1.0 / math.sqrt(rows * ctx_count * data_count))
    shard = lax.psum_scatter(stage, "dp", scatter_dimension=0, tiled=True).reshape(split, width)
    weight_grad = lax.all_gather(shard.astype(jnp.bfloat16), "ctx", axis=0, tiled=True).astype(
        jnp.float32
    )
    back_rows = back.reshape(blocks, BLK, HEADS, DH)
    dprobs = jnp.einsum(
        "qrhd,qkhd->qhrk", back_rows, picked_values, preferred_element_type=jnp.float32
    )
    delta = jnp.einsum("qrhd,qrhd->qhr", back_rows, attention, preferred_element_type=jnp.float32)[
        ..., None
    ]
    dscores = (probs * (dprobs - delta)).astype(jnp.bfloat16)
    query_sum = (
        jnp.einsum("qhrk,qkhd->qrhd", dscores, picked_keys, preferred_element_type=jnp.float32)
        * scale
    )
    query_grad = query_sum.astype(jnp.bfloat16).reshape(rows, width)
    return (mixed[None], query_grad[None], weight_grad)


def solution(mesh):
    return jax.shard_map(
        local,
        mesh=mesh,
        in_specs=(
            P("dp", "ctx", None),
            P("dp", "ctx", None),
            P("dp", "ctx", None),
            P("dp", "ctx", None),
            P("dp", None),
            P("dp", "ctx", None),
        ),
        out_specs=(P("dp", "ctx", None), P("dp", "ctx", None), P("dp", None)),
        check_vma=False,
    )
```

```python
import math

import jax
import jax.numpy as jnp
from jax import lax
from jax.experimental import pallas as pl
from jax.experimental.pallas import tpu as pltpu
from jax.sharding import PartitionSpec as P

HEADS = 16
DH = 128
BLK = 128
KSEL = 2


def _fwd_kernel(table, q_ref, k0_ref, k1_ref, v0_ref, v1_ref, att_ref, probs_ref):
    scale = 1.0 / math.sqrt(DH)
    for h in range(HEADS):
        lanes = slice(h * DH, (h + 1) * DH)
        keys = jnp.concatenate([k0_ref[0, :, lanes], k1_ref[0, :, lanes]], axis=0)
        scores = lax.dot_general(
            q_ref[:, lanes], keys, (((1,), (1,)), ((), ())), preferred_element_type=jnp.float32
        ) * scale
        top = jnp.max(scores, axis=-1, keepdims=True)
        weights = jnp.exp(scores - top)
        probs = weights / jnp.sum(weights, axis=-1, keepdims=True)
        vals = jnp.concatenate([v0_ref[0, :, lanes], v1_ref[0, :, lanes]], axis=0)
        att = jnp.dot(probs.astype(jnp.bfloat16), vals, preferred_element_type=jnp.float32)
        att_ref[:, lanes] = att.astype(att_ref.dtype)
        probs_ref[0, h] = probs


def forward_attention(query_flat, got, order):
    rows, width = query_flat.shape
    blocks = rows // BLK
    heads = width // DH

    def kv(k, off):
        return pl.BlockSpec((1, BLK, width), lambda b, t: (t[KSEL * b + k], 0, off))

    grid_spec = pltpu.PrefetchScalarGridSpec(
        num_scalar_prefetch=1,
        grid=(blocks,),
        in_specs=[
            pl.BlockSpec((BLK, width), lambda b, t: (b, 0)),
            kv(0, 0),
            kv(1, 0),
            kv(0, 1),
            kv(1, 1),
        ],
        out_specs=[
            pl.BlockSpec((BLK, width), lambda b, t: (b, 0)),
            pl.BlockSpec((1, heads, BLK, KSEL * BLK), lambda b, t: (b, 0, 0, 0)),
        ],
    )
    flops = blocks * heads * 4 * BLK * KSEL * BLK * DH
    return pl.pallas_call(
        _fwd_kernel,
        grid_spec=grid_spec,
        out_shape=[
            jax.ShapeDtypeStruct((rows, width), jnp.bfloat16),
            jax.ShapeDtypeStruct((blocks, heads, BLK, KSEL * BLK), jnp.float32),
        ],
        cost_estimate=pl.CostEstimate(
            flops=flops,
            transcendentals=blocks * heads * BLK * KSEL * BLK,
            bytes_accessed=rows * width * 2 * 6 + blocks * heads * BLK * KSEL * BLK * 4,
        ),
    )(order, query_flat, got, got, got, got)


def softmax_rows(scores):
    top = jnp.max(scores, axis=-1, keepdims=True)
    weights = jnp.exp(scores - top)
    return weights / jnp.sum(weights, axis=-1, keepdims=True)


def local(queries, keys, values, grad_out, out_weight, pattern):
    ctx_count = lax.axis_size("ctx")
    data_count = lax.axis_size("dp")
    own_index = lax.axis_index("ctx")
    rows = queries.shape[1]
    blocks = rows // BLK
    width = HEADS * DH
    scale = 1.0 / math.sqrt(DH)
    query_rows = queries[0].reshape(blocks, BLK, HEADS, DH)
    key_blocks = keys[0].reshape(blocks, BLK, width)
    value_blocks = values[0].reshape(blocks, BLK, width)
    table = pattern[0]
    owner = table // blocks
    every_table = lax.all_gather(table, "ctx", axis=0, tiled=True).reshape(ctx_count, blocks * KSEL)
    wanted = every_table // blocks == own_index
    send_index = jnp.sum(jnp.where(wanted, every_table % blocks, 0), axis=1)
    got = lax.all_to_all(
        jnp.concatenate(
            [jnp.take(key_blocks, send_index, axis=0), jnp.take(value_blocks, send_index, axis=0)],
            axis=-1,
        ),
        "ctx",
        split_axis=0,
        concat_axis=0,
        tiled=True,
    )
    got_keys, got_values = got[..., :width], got[..., width:]
    order = owner.reshape(-1)
    attention_flat, probs = forward_attention(queries[0], got, order)
    attention = attention_flat.reshape(blocks, BLK, HEADS, DH)
    picked_keys = jnp.take(got_keys, order, axis=0).reshape(blocks, KSEL * BLK, HEADS, DH)
    picked_values = jnp.take(got_values, order, axis=0).reshape(blocks, KSEL * BLK, HEADS, DH)
    grad_flat = grad_out[0]
    half = out_weight.shape[1] // 2
    side = own_index % 2
    own_half = lax.dynamic_slice_in_dim(out_weight, side * half, half, axis=1)
    own_half, attention_flat = lax.optimization_barrier((own_half, attention_flat))
    mine = lax.all_to_all(
        jnp.broadcast_to(own_half[None], (data_count,) + own_half.shape),
        "dp",
        split_axis=0,
        concat_axis=0,
        tiled=True,
    ).reshape(data_count * own_half.shape[0], half)
    other = lax.ppermute(mine, "ctx", [(j, j ^ 1) for j in range(ctx_count)])
    first = jnp.where(side == 0, mine, other)
    second = jnp.where(side == 0, other, mine)
    mixed_sum = jnp.concatenate(
        [
            jnp.dot(attention_flat, first, preferred_element_type=jnp.float32),
            jnp.dot(attention_flat, second, preferred_element_type=jnp.float32),
        ],
        axis=1,
    )
    dims = (((1,), (1,)), ((), ()))
    back_sum = lax.dot_general(
        grad_flat[:, :half], first, dims, preferred_element_type=jnp.float32
    ) + lax.dot_general(grad_flat[:, half:], second, dims, preferred_element_type=jnp.float32)
    mixed = mixed_sum.astype(jnp.bfloat16)
    back = back_sum.astype(jnp.bfloat16)
    split = width // (ctx_count * data_count)
    columns = (
        attention_flat.reshape(rows, data_count, ctx_count, split)
        .transpose(0, 2, 1, 3)
        .reshape(rows, width)
    )
    partial = lax.dot_general(
        columns, grad_flat, (((0,), (0,)), ((), ())), preferred_element_type=jnp.float32
    )
    stage = lax.psum_scatter(partial, "ctx", scatter_dimension=0, tiled=True)
    stage = stage * (1.0 / math.sqrt(rows * ctx_count * data_count))
    shard = jnp.sum(
        lax.all_to_all(
            stage.reshape(data_count, split, width), "dp", split_axis=0, concat_axis=0, tiled=True
        ),
        axis=0,
    )
    piece = shard.astype(jnp.bfloat16)
    weight_grad = lax.all_to_all(
        jnp.broadcast_to(piece[None], (ctx_count,) + piece.shape),
        "ctx",
        split_axis=0,
        concat_axis=0,
        tiled=True,
    ).reshape(ctx_count * split, width).astype(jnp.float32)
    back_rows = back.reshape(blocks, BLK, HEADS, DH)
    dprobs = jnp.einsum(
        "qrhd,qkhd->qhrk", back_rows, picked_values, preferred_element_type=jnp.float32
    )
    delta = jnp.einsum("qrhd,qrhd->qhr", back_rows, attention, preferred_element_type=jnp.float32)[
        ..., None
    ]
    dscores = (probs * (dprobs - delta)).astype(jnp.bfloat16)
    query_sum = (
        jnp.einsum("qhrk,qkhd->qrhd", dscores, picked_keys, preferred_element_type=jnp.float32)
        * scale
    )
    query_grad = query_sum.astype(jnp.bfloat16).reshape(rows, width)
    return (mixed[None], query_grad[None], weight_grad)


def solution(mesh):
    return jax.shard_map(
        local,
        mesh=mesh,
        in_specs=(
            P("dp", "ctx", None),
            P("dp", "ctx", None),
            P("dp", "ctx", None),
            P("dp", "ctx", None),
            P("dp", None),
            P("dp", "ctx", None),
        ),
        out_specs=(P("dp", "ctx", None), P("dp", "ctx", None), P("dp", None)),
        check_vma=False,
    )
```

```python
import math

import jax
import jax.numpy as jnp
from jax import lax
from jax.experimental import pallas as pl
from jax.experimental.pallas import tpu as pltpu
from jax.sharding import PartitionSpec as P

HEADS = 16
DH = 128
BLK = 128
KSEL = 2


def _fwd_kernel(table, q_ref, k0_ref, k1_ref, v0_ref, v1_ref, att_ref, probs_ref):
    scale = 1.0 / math.sqrt(DH)
    for h in range(HEADS):
        lanes = slice(h * DH, (h + 1) * DH)
        keys = jnp.concatenate([k0_ref[0, :, lanes], k1_ref[0, :, lanes]], axis=0)
        scores = lax.dot_general(
            q_ref[:, lanes], keys, (((1,), (1,)), ((), ())), preferred_element_type=jnp.float32
        ) * scale
        top = jnp.max(scores, axis=-1, keepdims=True)
        weights = jnp.exp(scores - top)
        probs = weights / jnp.sum(weights, axis=-1, keepdims=True)
        vals = jnp.concatenate([v0_ref[0, :, lanes], v1_ref[0, :, lanes]], axis=0)
        att = jnp.dot(probs.astype(jnp.bfloat16), vals, preferred_element_type=jnp.float32)
        att_ref[:, lanes] = att.astype(att_ref.dtype)
        probs_ref[0, h] = probs


def forward_attention(query_flat, got, order):
    rows, width = query_flat.shape
    blocks = rows // BLK
    heads = width // DH

    def kv(k, off):
        return pl.BlockSpec((1, BLK, width), lambda b, t: (t[KSEL * b + k], 0, off))

    grid_spec = pltpu.PrefetchScalarGridSpec(
        num_scalar_prefetch=1,
        grid=(blocks,),
        in_specs=[
            pl.BlockSpec((BLK, width), lambda b, t: (b, 0)),
            kv(0, 0),
            kv(1, 0),
            kv(0, 1),
            kv(1, 1),
        ],
        out_specs=[
            pl.BlockSpec((BLK, width), lambda b, t: (b, 0)),
            pl.BlockSpec((1, heads, BLK, KSEL * BLK), lambda b, t: (b, 0, 0, 0)),
        ],
    )
    flops = blocks * heads * 4 * BLK * KSEL * BLK * DH
    return pl.pallas_call(
        _fwd_kernel,
        grid_spec=grid_spec,
        out_shape=[
            jax.ShapeDtypeStruct((rows, width), jnp.bfloat16),
            jax.ShapeDtypeStruct((blocks, heads, BLK, KSEL * BLK), jnp.float32),
        ],
        cost_estimate=pl.CostEstimate(
            flops=flops,
            transcendentals=blocks * heads * BLK * KSEL * BLK,
            bytes_accessed=rows * width * 2 * 6 + blocks * heads * BLK * KSEL * BLK * 4,
        ),
    )(order, query_flat, got, got, got, got)


def _send_kernel(index, k_ref, v_ref, o_ref):
    width = k_ref.shape[-1]
    o_ref[0, :, :width] = k_ref[0]
    o_ref[0, :, width:] = v_ref[0]


def send_buffer(key_blocks, value_blocks, send_index):
    count = send_index.shape[0]
    _, blk, width = key_blocks.shape
    grid_spec = pltpu.PrefetchScalarGridSpec(
        num_scalar_prefetch=1,
        grid=(count,),
        in_specs=[
            pl.BlockSpec((1, blk, width), lambda d, t: (t[d], 0, 0)),
            pl.BlockSpec((1, blk, width), lambda d, t: (t[d], 0, 0)),
        ],
        out_specs=pl.BlockSpec((1, blk, 2 * width), lambda d, t: (d, 0, 0)),
    )
    return pl.pallas_call(
        _send_kernel,
        grid_spec=grid_spec,
        out_shape=jax.ShapeDtypeStruct((count, blk, 2 * width), key_blocks.dtype),
        cost_estimate=pl.CostEstimate(flops=0, transcendentals=0, bytes_accessed=count * blk * width * 8),
    )(send_index, key_blocks, value_blocks)


def softmax_rows(scores):
    top = jnp.max(scores, axis=-1, keepdims=True)
    weights = jnp.exp(scores - top)
    return weights / jnp.sum(weights, axis=-1, keepdims=True)


def local(queries, keys, values, grad_out, out_weight, pattern):
    ctx_count = lax.axis_size("ctx")
    data_count = lax.axis_size("dp")
    own_index = lax.axis_index("ctx")
    rows = queries.shape[1]
    blocks = rows // BLK
    width = HEADS * DH
    scale = 1.0 / math.sqrt(DH)
    query_rows = queries[0].reshape(blocks, BLK, HEADS, DH)
    key_blocks = keys[0].reshape(blocks, BLK, width)
    value_blocks = values[0].reshape(blocks, BLK, width)
    table = pattern[0]
    owner = table // blocks
    flat_table = table.reshape(1, blocks * KSEL)
    every_table = lax.all_to_all(
        jnp.broadcast_to(flat_table, (ctx_count, blocks * KSEL)),
        "ctx",
        split_axis=0,
        concat_axis=0,
        tiled=True,
    )
    wanted = every_table // blocks == own_index
    send_index = jnp.sum(jnp.where(wanted, every_table % blocks, 0), axis=1)
    got = lax.all_to_all(
        send_buffer(key_blocks, value_blocks, send_index),
        "ctx",
        split_axis=0,
        concat_axis=0,
        tiled=True,
    )
    got_keys, got_values = got[..., :width], got[..., width:]
    order = owner.reshape(-1)
    attention_flat, probs = forward_attention(queries[0], got, order)
    attention = attention_flat.reshape(blocks, BLK, HEADS, DH)
    picked_keys = jnp.take(got_keys, order, axis=0).reshape(blocks, KSEL * BLK, HEADS, DH)
    picked_values = jnp.take(got_values, order, axis=0).reshape(blocks, KSEL * BLK, HEADS, DH)
    grad_flat = grad_out[0]
    half = out_weight.shape[1] // 2
    side = own_index % 2
    own_half = lax.dynamic_slice_in_dim(out_weight, side * half, half, axis=1)
    own_half, attention_flat = lax.optimization_barrier((own_half, attention_flat))
    mine = lax.all_to_all(
        jnp.broadcast_to(own_half[None], (data_count,) + own_half.shape),
        "dp",
        split_axis=0,
        concat_axis=0,
        tiled=True,
    ).reshape(data_count * own_half.shape[0], half)
    other = lax.ppermute(mine, "ctx", [(j, j ^ 1) for j in range(ctx_count)])
    first = jnp.where(side == 0, mine, other)
    second = jnp.where(side == 0, other, mine)
    mixed_sum = jnp.concatenate(
        [
            jnp.dot(attention_flat, first, preferred_element_type=jnp.float32),
            jnp.dot(attention_flat, second, preferred_element_type=jnp.float32),
        ],
        axis=1,
    )
    dims = (((1,), (1,)), ((), ()))
    back_sum = lax.dot_general(
        grad_flat[:, :half], first, dims, preferred_element_type=jnp.float32
    ) + lax.dot_general(grad_flat[:, half:], second, dims, preferred_element_type=jnp.float32)
    mixed = mixed_sum.astype(jnp.bfloat16)
    back = back_sum.astype(jnp.bfloat16)
    split = width // (ctx_count * data_count)
    columns = (
        attention_flat.reshape(rows, data_count, ctx_count, split)
        .transpose(0, 2, 1, 3)
        .reshape(rows, width)
    )
    partial = lax.dot_general(
        columns, grad_flat, (((0,), (0,)), ((), ())), preferred_element_type=jnp.float32
    )
    stage = lax.psum_scatter(partial, "ctx", scatter_dimension=0, tiled=True)
    stage = stage * (1.0 / math.sqrt(rows * ctx_count * data_count))
    shard = jnp.sum(
        lax.all_to_all(
            stage.reshape(data_count, split, width), "dp", split_axis=0, concat_axis=0, tiled=True
        ),
        axis=0,
    )
    piece = shard.astype(jnp.bfloat16)
    weight_grad = lax.all_to_all(
        jnp.broadcast_to(piece[None], (ctx_count,) + piece.shape),
        "ctx",
        split_axis=0,
        concat_axis=0,
        tiled=True,
    ).reshape(ctx_count * split, width).astype(jnp.float32)
    back_rows = back.reshape(blocks, BLK, HEADS, DH)
    dprobs = jnp.einsum(
        "qrhd,qkhd->qhrk", back_rows, picked_values, preferred_element_type=jnp.float32
    )
    delta = jnp.einsum("qrhd,qrhd->qhr", back_rows, attention, preferred_element_type=jnp.float32)[
        ..., None
    ]
    dscores = (probs * (dprobs - delta)).astype(jnp.bfloat16)
    query_sum = (
        jnp.einsum("qhrk,qkhd->qrhd", dscores, picked_keys, preferred_element_type=jnp.float32)
        * scale
    )
    query_grad = query_sum.astype(jnp.bfloat16).reshape(rows, width)
    return (mixed[None], query_grad[None], weight_grad)


def solution(mesh):
    return jax.shard_map(
        local,
        mesh=mesh,
        in_specs=(
            P("dp", "ctx", None),
            P("dp", "ctx", None),
            P("dp", "ctx", None),
            P("dp", "ctx", None),
            P("dp", None),
            P("dp", "ctx", None),
        ),
        out_specs=(P("dp", "ctx", None), P("dp", "ctx", None), P("dp", None)),
        check_vma=False,
    )
```

```python
import math

import jax
import jax.numpy as jnp
from jax import lax
from jax.experimental import pallas as pl
from jax.experimental.pallas import tpu as pltpu
from jax.sharding import PartitionSpec as P

HEADS = 16
DH = 128
BLK = 128
KSEL = 2


def _fwd_kernel(table, q_ref, k0_ref, k1_ref, v0_ref, v1_ref, att_ref, probs_ref):
    scale = 1.0 / math.sqrt(DH)
    for h in range(HEADS):
        lanes = slice(h * DH, (h + 1) * DH)
        keys = jnp.concatenate([k0_ref[0, :, lanes], k1_ref[0, :, lanes]], axis=0)
        scores = lax.dot_general(
            q_ref[:, lanes], keys, (((1,), (1,)), ((), ())), preferred_element_type=jnp.float32
        ) * scale
        top = jnp.max(scores, axis=-1, keepdims=True)
        weights = jnp.exp(scores - top)
        probs = weights / jnp.sum(weights, axis=-1, keepdims=True)
        vals = jnp.concatenate([v0_ref[0, :, lanes], v1_ref[0, :, lanes]], axis=0)
        att = jnp.dot(probs.astype(jnp.bfloat16), vals, preferred_element_type=jnp.float32)
        att_ref[:, lanes] = att.astype(att_ref.dtype)
        probs_ref[0, h] = probs


def forward_attention(query_flat, got, order):
    rows, width = query_flat.shape
    blocks = rows // BLK
    heads = width // DH

    def kv(k, off):
        return pl.BlockSpec((1, BLK, width), lambda b, t: (t[KSEL * b + k], 0, off))

    grid_spec = pltpu.PrefetchScalarGridSpec(
        num_scalar_prefetch=1,
        grid=(blocks,),
        in_specs=[
            pl.BlockSpec((BLK, width), lambda b, t: (b, 0)),
            kv(0, 0),
            kv(1, 0),
            kv(0, 1),
            kv(1, 1),
        ],
        out_specs=[
            pl.BlockSpec((BLK, width), lambda b, t: (b, 0)),
            pl.BlockSpec((1, heads, BLK, KSEL * BLK), lambda b, t: (b, 0, 0, 0)),
        ],
    )
    flops = blocks * heads * 4 * BLK * KSEL * BLK * DH
    return pl.pallas_call(
        _fwd_kernel,
        grid_spec=grid_spec,
        out_shape=[
            jax.ShapeDtypeStruct((rows, width), jnp.bfloat16),
            jax.ShapeDtypeStruct((blocks, heads, BLK, KSEL * BLK), jnp.float32),
        ],
        cost_estimate=pl.CostEstimate(
            flops=flops,
            transcendentals=blocks * heads * BLK * KSEL * BLK,
            bytes_accessed=rows * width * 2 * 6 + blocks * heads * BLK * KSEL * BLK * 4,
        ),
    )(order, query_flat, got, got, got, got)


def _bwd_kernel(table, back_ref, att_ref, probs_ref, k0_ref, k1_ref, v0_ref, v1_ref, out_ref):
    scale = 1.0 / math.sqrt(DH)
    for h in range(HEADS):
        lanes = slice(h * DH, (h + 1) * DH)
        back = back_ref[:, lanes]
        vals = jnp.concatenate([v0_ref[0, :, lanes], v1_ref[0, :, lanes]], axis=0)
        dprobs = lax.dot_general(
            back, vals, (((1,), (1,)), ((), ())), preferred_element_type=jnp.float32
        )
        delta = jnp.sum(
            back.astype(jnp.float32) * att_ref[:, lanes].astype(jnp.float32), axis=-1, keepdims=True
        )
        dscores = (probs_ref[0, h] * (dprobs - delta)).astype(jnp.bfloat16)
        keys = jnp.concatenate([k0_ref[0, :, lanes], k1_ref[0, :, lanes]], axis=0)
        grad = jnp.dot(dscores, keys, preferred_element_type=jnp.float32) * scale
        out_ref[:, lanes] = grad.astype(out_ref.dtype)


def backward_attention(back_flat, attention_flat, probs, got, order):
    rows, width = back_flat.shape
    blocks = rows // BLK
    heads = width // DH

    def kv(k, off):
        return pl.BlockSpec((1, BLK, width), lambda b, t: (t[KSEL * b + k], 0, off))

    grid_spec = pltpu.PrefetchScalarGridSpec(
        num_scalar_prefetch=1,
        grid=(blocks,),
        in_specs=[
            pl.BlockSpec((BLK, width), lambda b, t: (b, 0)),
            pl.BlockSpec((BLK, width), lambda b, t: (b, 0)),
            pl.BlockSpec((1, heads, BLK, KSEL * BLK), lambda b, t: (b, 0, 0, 0)),
            kv(0, 0),
            kv(1, 0),
            kv(0, 1),
            kv(1, 1),
        ],
        out_specs=pl.BlockSpec((BLK, width), lambda b, t: (b, 0)),
    )
    flops = blocks * heads * 4 * BLK * KSEL * BLK * DH
    return pl.pallas_call(
        _bwd_kernel,
        grid_spec=grid_spec,
        out_shape=jax.ShapeDtypeStruct((rows, width), jnp.bfloat16),
        cost_estimate=pl.CostEstimate(
            flops=flops,
            transcendentals=0,
            bytes_accessed=rows * width * 2 * 7 + blocks * heads * BLK * KSEL * BLK * 4,
        ),
    )(order, back_flat, attention_flat, probs, got, got, got, got)


def _send_kernel(index, k_ref, v_ref, o_ref):
    width = k_ref.shape[-1]
    o_ref[0, :, :width] = k_ref[0]
    o_ref[0, :, width:] = v_ref[0]


def send_buffer(key_blocks, value_blocks, send_index):
    count = send_index.shape[0]
    _, blk, width = key_blocks.shape
    grid_spec = pltpu.PrefetchScalarGridSpec(
        num_scalar_prefetch=1,
        grid=(count,),
        in_specs=[
            pl.BlockSpec((1, blk, width), lambda d, t: (t[d], 0, 0)),
            pl.BlockSpec((1, blk, width), lambda d, t: (t[d], 0, 0)),
        ],
        out_specs=pl.BlockSpec((1, blk, 2 * width), lambda d, t: (d, 0, 0)),
    )
    return pl.pallas_call(
        _send_kernel,
        grid_spec=grid_spec,
        out_shape=jax.ShapeDtypeStruct((count, blk, 2 * width), key_blocks.dtype),
        cost_estimate=pl.CostEstimate(flops=0, transcendentals=0, bytes_accessed=count * blk * width * 8),
    )(send_index, key_blocks, value_blocks)


def softmax_rows(scores):
    top = jnp.max(scores, axis=-1, keepdims=True)
    weights = jnp.exp(scores - top)
    return weights / jnp.sum(weights, axis=-1, keepdims=True)


def local(queries, keys, values, grad_out, out_weight, pattern):
    ctx_count = lax.axis_size("ctx")
    data_count = lax.axis_size("dp")
    own_index = lax.axis_index("ctx")
    rows = queries.shape[1]
    blocks = rows // BLK
    width = HEADS * DH
    scale = 1.0 / math.sqrt(DH)
    key_blocks = keys[0].reshape(blocks, BLK, width)
    value_blocks = values[0].reshape(blocks, BLK, width)
    table = pattern[0]
    owner = table // blocks
    flat_table = table.reshape(1, blocks * KSEL)
    every_table = lax.all_to_all(
        jnp.broadcast_to(flat_table, (ctx_count, blocks * KSEL)),
        "ctx",
        split_axis=0,
        concat_axis=0,
        tiled=True,
    )
    wanted = every_table // blocks == own_index
    send_index = jnp.sum(jnp.where(wanted, every_table % blocks, 0), axis=1)
    got = lax.all_to_all(
        send_buffer(key_blocks, value_blocks, send_index),
        "ctx",
        split_axis=0,
        concat_axis=0,
        tiled=True,
    )
    order = owner.reshape(-1)
    attention_flat, probs = forward_attention(queries[0], got, order)
    grad_flat = grad_out[0]
    half = out_weight.shape[1] // 2
    side = own_index % 2
    own_half = lax.dynamic_slice_in_dim(out_weight, side * half, half, axis=1)
    own_half, attention_flat = lax.optimization_barrier((own_half, attention_flat))
    mine = lax.all_to_all(
        jnp.broadcast_to(own_half[None], (data_count,) + own_half.shape),
        "dp",
        split_axis=0,
        concat_axis=0,
        tiled=True,
    ).reshape(data_count * own_half.shape[0], half)
    other = lax.ppermute(mine, "ctx", [(j, j ^ 1) for j in range(ctx_count)])
    first = jnp.where(side == 0, mine, other)
    second = jnp.where(side == 0, other, mine)
    mixed_sum = jnp.concatenate(
        [
            jnp.dot(attention_flat, first, preferred_element_type=jnp.float32),
            jnp.dot(attention_flat, second, preferred_element_type=jnp.float32),
        ],
        axis=1,
    )
    dims = (((1,), (1,)), ((), ()))
    back_sum = lax.dot_general(
        grad_flat[:, :half], first, dims, preferred_element_type=jnp.float32
    ) + lax.dot_general(grad_flat[:, half:], second, dims, preferred_element_type=jnp.float32)
    mixed = mixed_sum.astype(jnp.bfloat16)
    back = back_sum.astype(jnp.bfloat16)
    split = width // (ctx_count * data_count)
    columns = (
        attention_flat.reshape(rows, data_count, ctx_count, split)
        .transpose(0, 2, 1, 3)
        .reshape(rows, width)
    )
    partial = lax.dot_general(
        columns, grad_flat, (((0,), (0,)), ((), ())), preferred_element_type=jnp.float32
    )
    stage = lax.psum_scatter(partial, "ctx", scatter_dimension=0, tiled=True)
    stage = stage * (1.0 / math.sqrt(rows * ctx_count * data_count))
    shard = jnp.sum(
        lax.all_to_all(
            stage.reshape(data_count, split, width), "dp", split_axis=0, concat_axis=0, tiled=True
        ),
        axis=0,
    )
    piece = shard.astype(jnp.bfloat16)
    weight_grad = lax.all_to_all(
        jnp.broadcast_to(piece[None], (ctx_count,) + piece.shape),
        "ctx",
        split_axis=0,
        concat_axis=0,
        tiled=True,
    ).reshape(ctx_count * split, width).astype(jnp.float32)
    query_grad = backward_attention(back, attention_flat, probs, got, order)
    return (mixed[None], query_grad[None], weight_grad)


def solution(mesh):
    return jax.shard_map(
        local,
        mesh=mesh,
        in_specs=(
            P("dp", "ctx", None),
            P("dp", "ctx", None),
            P("dp", "ctx", None),
            P("dp", "ctx", None),
            P("dp", None),
            P("dp", "ctx", None),
        ),
        out_specs=(P("dp", "ctx", None), P("dp", "ctx", None), P("dp", None)),
        check_vma=False,
    )
```

```python
import math

import jax
import jax.numpy as jnp
from jax import lax
from jax.experimental import pallas as pl
from jax.experimental.pallas import tpu as pltpu
from jax.sharding import PartitionSpec as P

HEADS = 16
DH = 128
BLK = 128
KSEL = 2


def _fwd_kernel(table, q_ref, k0_ref, k1_ref, v0_ref, v1_ref, att_ref, probs_ref):
    scale = 1.0 / math.sqrt(DH)
    for h in range(HEADS):
        lanes = slice(h * DH, (h + 1) * DH)
        keys = jnp.concatenate([k0_ref[0, :, lanes], k1_ref[0, :, lanes]], axis=0)
        scores = lax.dot_general(
            q_ref[:, lanes], keys, (((1,), (1,)), ((), ())), preferred_element_type=jnp.float32
        ) * scale
        top = jnp.max(scores, axis=-1, keepdims=True)
        weights = jnp.exp(scores - top)
        probs = weights / jnp.sum(weights, axis=-1, keepdims=True)
        vals = jnp.concatenate([v0_ref[0, :, lanes], v1_ref[0, :, lanes]], axis=0)
        att = jnp.dot(probs.astype(jnp.bfloat16), vals, preferred_element_type=jnp.float32)
        att_ref[:, lanes] = att.astype(att_ref.dtype)
        probs_ref[0, h] = probs


def forward_attention(query_flat, got, order):
    rows, width = query_flat.shape
    blocks = rows // BLK
    heads = width // DH

    def kv(k, off):
        return pl.BlockSpec((1, BLK, width), lambda b, t: (t[KSEL * b + k], 0, off))

    grid_spec = pltpu.PrefetchScalarGridSpec(
        num_scalar_prefetch=1,
        grid=(blocks,),
        in_specs=[
            pl.BlockSpec((BLK, width), lambda b, t: (b, 0)),
            kv(0, 0),
            kv(1, 0),
            kv(0, 1),
            kv(1, 1),
        ],
        out_specs=[
            pl.BlockSpec((BLK, width), lambda b, t: (b, 0)),
            pl.BlockSpec((1, heads, BLK, KSEL * BLK), lambda b, t: (b, 0, 0, 0)),
        ],
    )
    flops = blocks * heads * 4 * BLK * KSEL * BLK * DH
    return pl.pallas_call(
        _fwd_kernel,
        grid_spec=grid_spec,
        out_shape=[
            jax.ShapeDtypeStruct((rows, width), jnp.bfloat16),
            jax.ShapeDtypeStruct((blocks, heads, BLK, KSEL * BLK), jnp.float32),
        ],
        cost_estimate=pl.CostEstimate(
            flops=flops,
            transcendentals=blocks * heads * BLK * KSEL * BLK,
            bytes_accessed=rows * width * 2 * 6 + blocks * heads * BLK * KSEL * BLK * 4,
        ),
    )(order, query_flat, got, got, got, got)


def _bwd_kernel(table, back_ref, att_ref, probs_ref, k0_ref, k1_ref, v0_ref, v1_ref, out_ref):
    scale = 1.0 / math.sqrt(DH)
    for h in range(HEADS):
        lanes = slice(h * DH, (h + 1) * DH)
        back = back_ref[:, lanes]
        vals = jnp.concatenate([v0_ref[0, :, lanes], v1_ref[0, :, lanes]], axis=0)
        dprobs = lax.dot_general(
            back, vals, (((1,), (1,)), ((), ())), preferred_element_type=jnp.float32
        )
        delta = jnp.sum(
            back.astype(jnp.float32) * att_ref[:, lanes].astype(jnp.float32), axis=-1, keepdims=True
        )
        dscores = (probs_ref[0, h] * (dprobs - delta)).astype(jnp.bfloat16)
        keys = jnp.concatenate([k0_ref[0, :, lanes], k1_ref[0, :, lanes]], axis=0)
        grad = jnp.dot(dscores, keys, preferred_element_type=jnp.float32) * scale
        out_ref[:, lanes] = grad.astype(out_ref.dtype)


def backward_attention(back_flat, attention_flat, probs, got, order):
    rows, width = back_flat.shape
    blocks = rows // BLK
    heads = width // DH

    def kv(k, off):
        return pl.BlockSpec((1, BLK, width), lambda b, t: (t[KSEL * b + k], 0, off))

    grid_spec = pltpu.PrefetchScalarGridSpec(
        num_scalar_prefetch=1,
        grid=(blocks,),
        in_specs=[
            pl.BlockSpec((BLK, width), lambda b, t: (b, 0)),
            pl.BlockSpec((BLK, width), lambda b, t: (b, 0)),
            pl.BlockSpec((1, heads, BLK, KSEL * BLK), lambda b, t: (b, 0, 0, 0)),
            kv(0, 0),
            kv(1, 0),
            kv(0, 1),
            kv(1, 1),
        ],
        out_specs=pl.BlockSpec((BLK, width), lambda b, t: (b, 0)),
    )
    flops = blocks * heads * 4 * BLK * KSEL * BLK * DH
    return pl.pallas_call(
        _bwd_kernel,
        grid_spec=grid_spec,
        out_shape=jax.ShapeDtypeStruct((rows, width), jnp.bfloat16),
        cost_estimate=pl.CostEstimate(
            flops=flops,
            transcendentals=0,
            bytes_accessed=rows * width * 2 * 7 + blocks * heads * BLK * KSEL * BLK * 4,
        ),
    )(order, back_flat, attention_flat, probs, got, got, got, got)


def _send_kernel(index, k_ref, v_ref, o_ref):
    width = k_ref.shape[-1]
    o_ref[0, :, :width] = k_ref[0]
    o_ref[0, :, width:] = v_ref[0]


def send_buffer(key_blocks, value_blocks, send_index):
    count = send_index.shape[0]
    _, blk, width = key_blocks.shape
    grid_spec = pltpu.PrefetchScalarGridSpec(
        num_scalar_prefetch=1,
        grid=(count,),
        in_specs=[
            pl.BlockSpec((1, blk, width), lambda d, t: (t[d], 0, 0)),
            pl.BlockSpec((1, blk, width), lambda d, t: (t[d], 0, 0)),
        ],
        out_specs=pl.BlockSpec((1, blk, 2 * width), lambda d, t: (d, 0, 0)),
    )
    return pl.pallas_call(
        _send_kernel,
        grid_spec=grid_spec,
        out_shape=jax.ShapeDtypeStruct((count, blk, 2 * width), key_blocks.dtype),
        cost_estimate=pl.CostEstimate(flops=0, transcendentals=0, bytes_accessed=count * blk * width * 8),
    )(send_index, key_blocks, value_blocks)


def softmax_rows(scores):
    top = jnp.max(scores, axis=-1, keepdims=True)
    weights = jnp.exp(scores - top)
    return weights / jnp.sum(weights, axis=-1, keepdims=True)


def local(queries, keys, values, grad_out, out_weight, pattern):
    ctx_count = lax.axis_size("ctx")
    data_count = lax.axis_size("dp")
    own_index = lax.axis_index("ctx")
    rows = queries.shape[1]
    blocks = rows // BLK
    width = HEADS * DH
    scale = 1.0 / math.sqrt(DH)
    key_blocks = keys[0].reshape(blocks, BLK, width)
    value_blocks = values[0].reshape(blocks, BLK, width)
    table = pattern[0]
    owner = table // blocks
    flat_table = table.reshape(1, blocks * KSEL)
    every_table = lax.all_to_all(
        jnp.broadcast_to(flat_table, (ctx_count, blocks * KSEL)),
        "ctx",
        split_axis=0,
        concat_axis=0,
        tiled=True,
    )
    wanted = every_table // blocks == own_index
    send_index = jnp.sum(jnp.where(wanted, every_table % blocks, 0), axis=1)
    got = lax.all_to_all(
        send_buffer(key_blocks, value_blocks, send_index),
        "ctx",
        split_axis=0,
        concat_axis=0,
        tiled=True,
    )
    order = owner.reshape(-1)
    attention_flat, probs = forward_attention(queries[0], got, order)
    grad_flat = grad_out[0]
    half = out_weight.shape[1] // 2
    side = own_index % 2
    own_half = lax.dynamic_slice_in_dim(out_weight, side * half, half, axis=1)
    own_half, attention_flat = lax.optimization_barrier((own_half, attention_flat))
    mine = lax.all_to_all(
        jnp.broadcast_to(own_half[None], (data_count,) + own_half.shape),
        "dp",
        split_axis=0,
        concat_axis=0,
        tiled=True,
    ).reshape(data_count * own_half.shape[0], half)
    other = lax.ppermute(mine, "ctx", [(j, j ^ 1) for j in range(ctx_count)])
    first = jnp.where(side == 0, mine, other)
    second = jnp.where(side == 0, other, mine)
    mixed_sum = jnp.concatenate(
        [
            jnp.dot(attention_flat, first, preferred_element_type=jnp.float32),
            jnp.dot(attention_flat, second, preferred_element_type=jnp.float32),
        ],
        axis=1,
    )
    dims = (((1,), (1,)), ((), ()))
    back_sum = lax.dot_general(
        grad_flat[:, :half], first, dims, preferred_element_type=jnp.float32
    ) + lax.dot_general(grad_flat[:, half:], second, dims, preferred_element_type=jnp.float32)
    mixed = mixed_sum.astype(jnp.bfloat16)
    back = back_sum.astype(jnp.bfloat16)
    split = width // (ctx_count * data_count)
    columns = (
        attention_flat.reshape(rows, data_count, ctx_count, split)
        .transpose(0, 2, 1, 3)
        .reshape(rows, width)
    )
    partial = lax.dot_general(
        columns, grad_flat, (((0,), (0,)), ((), ())), preferred_element_type=jnp.float32
    )
    stage = lax.psum_scatter(partial, "ctx", scatter_dimension=0, tiled=True)
    query_grad = backward_attention(back, attention_flat, probs, got, order)
    stage, mixed, query_grad = lax.optimization_barrier((stage, mixed, query_grad))
    stage = stage * (1.0 / math.sqrt(rows * ctx_count * data_count))
    shard = jnp.sum(
        lax.all_to_all(
            stage.reshape(data_count, split, width), "dp", split_axis=0, concat_axis=0, tiled=True
        ),
        axis=0,
    )
    piece = shard.astype(jnp.bfloat16)
    weight_grad = lax.all_to_all(
        jnp.broadcast_to(piece[None], (ctx_count,) + piece.shape),
        "ctx",
        split_axis=0,
        concat_axis=0,
        tiled=True,
    ).reshape(ctx_count * split, width).astype(jnp.float32)
    return (mixed[None], query_grad[None], weight_grad)


def solution(mesh):
    return jax.shard_map(
        local,
        mesh=mesh,
        in_specs=(
            P("dp", "ctx", None),
            P("dp", "ctx", None),
            P("dp", "ctx", None),
            P("dp", "ctx", None),
            P("dp", None),
            P("dp", "ctx", None),
        ),
        out_specs=(P("dp", "ctx", None), P("dp", "ctx", None), P("dp", None)),
        check_vma=False,
    )
```

```python
import math

import jax
import jax.numpy as jnp
from jax import lax
from jax.experimental import pallas as pl
from jax.experimental.pallas import tpu as pltpu
from jax.sharding import PartitionSpec as P

HEADS = 16
DH = 128
BLK = 128
KSEL = 2


def _fwd_kernel(table, q_ref, k0_ref, k1_ref, v0_ref, v1_ref, att_ref, probs_ref):
    scale = 1.0 / math.sqrt(DH)
    for h in range(HEADS):
        lanes = slice(h * DH, (h + 1) * DH)
        keys = jnp.concatenate([k0_ref[0, :, lanes], k1_ref[0, :, lanes]], axis=0)
        scores = lax.dot_general(
            q_ref[:, lanes], keys, (((1,), (1,)), ((), ())), preferred_element_type=jnp.float32
        ) * scale
        top = jnp.max(scores, axis=-1, keepdims=True)
        weights = jnp.exp(scores - top)
        probs = weights / jnp.sum(weights, axis=-1, keepdims=True)
        vals = jnp.concatenate([v0_ref[0, :, lanes], v1_ref[0, :, lanes]], axis=0)
        att = jnp.dot(probs.astype(jnp.bfloat16), vals, preferred_element_type=jnp.float32)
        att_ref[:, lanes] = att.astype(att_ref.dtype)
        probs_ref[0, h] = probs


def forward_attention(query_flat, got, order):
    rows, width = query_flat.shape
    blocks = rows // BLK
    heads = width // DH

    def kv(k, off):
        return pl.BlockSpec((1, BLK, width), lambda b, t: (t[KSEL * b + k], 0, off))

    grid_spec = pltpu.PrefetchScalarGridSpec(
        num_scalar_prefetch=1,
        grid=(blocks,),
        in_specs=[
            pl.BlockSpec((BLK, width), lambda b, t: (b, 0)),
            kv(0, 0),
            kv(1, 0),
            kv(0, 1),
            kv(1, 1),
        ],
        out_specs=[
            pl.BlockSpec((BLK, width), lambda b, t: (b, 0)),
            pl.BlockSpec((1, heads, BLK, KSEL * BLK), lambda b, t: (b, 0, 0, 0)),
        ],
    )
    flops = blocks * heads * 4 * BLK * KSEL * BLK * DH
    return pl.pallas_call(
        _fwd_kernel,
        grid_spec=grid_spec,
        out_shape=[
            jax.ShapeDtypeStruct((rows, width), jnp.bfloat16),
            jax.ShapeDtypeStruct((blocks, heads, BLK, KSEL * BLK), jnp.float32),
        ],
        cost_estimate=pl.CostEstimate(
            flops=flops,
            transcendentals=blocks * heads * BLK * KSEL * BLK,
            bytes_accessed=rows * width * 2 * 6 + blocks * heads * BLK * KSEL * BLK * 4,
        ),
    )(order, query_flat, got, got, got, got)


def _bwd_kernel(table, back_ref, att_ref, probs_ref, k0_ref, k1_ref, v0_ref, v1_ref, out_ref):
    scale = 1.0 / math.sqrt(DH)
    for h in range(HEADS):
        lanes = slice(h * DH, (h + 1) * DH)
        back = back_ref[:, lanes]
        vals = jnp.concatenate([v0_ref[0, :, lanes], v1_ref[0, :, lanes]], axis=0)
        dprobs = lax.dot_general(
            back, vals, (((1,), (1,)), ((), ())), preferred_element_type=jnp.float32
        )
        delta = jnp.sum(
            back.astype(jnp.float32) * att_ref[:, lanes].astype(jnp.float32), axis=-1, keepdims=True
        )
        dscores = (probs_ref[0, h] * (dprobs - delta)).astype(jnp.bfloat16)
        keys = jnp.concatenate([k0_ref[0, :, lanes], k1_ref[0, :, lanes]], axis=0)
        grad = jnp.dot(dscores, keys, preferred_element_type=jnp.float32) * scale
        out_ref[:, lanes] = grad.astype(out_ref.dtype)


def backward_attention(back_flat, attention_flat, probs, got, order):
    rows, width = back_flat.shape
    blocks = rows // BLK
    heads = width // DH

    def kv(k, off):
        return pl.BlockSpec((1, BLK, width), lambda b, t: (t[KSEL * b + k], 0, off))

    grid_spec = pltpu.PrefetchScalarGridSpec(
        num_scalar_prefetch=1,
        grid=(blocks,),
        in_specs=[
            pl.BlockSpec((BLK, width), lambda b, t: (b, 0)),
            pl.BlockSpec((BLK, width), lambda b, t: (b, 0)),
            pl.BlockSpec((1, heads, BLK, KSEL * BLK), lambda b, t: (b, 0, 0, 0)),
            kv(0, 0),
            kv(1, 0),
            kv(0, 1),
            kv(1, 1),
        ],
        out_specs=pl.BlockSpec((BLK, width), lambda b, t: (b, 0)),
    )
    flops = blocks * heads * 4 * BLK * KSEL * BLK * DH
    return pl.pallas_call(
        _bwd_kernel,
        grid_spec=grid_spec,
        out_shape=jax.ShapeDtypeStruct((rows, width), jnp.bfloat16),
        cost_estimate=pl.CostEstimate(
            flops=flops,
            transcendentals=0,
            bytes_accessed=rows * width * 2 * 7 + blocks * heads * BLK * KSEL * BLK * 4,
        ),
    )(order, back_flat, attention_flat, probs, got, got, got, got)


def _send_kernel(index, k0_ref, k1_ref, v0_ref, v1_ref, o_ref):
    width = k0_ref.shape[-1]
    o_ref[0, :, :width] = k0_ref[0]
    o_ref[0, :, width:] = v0_ref[0]
    o_ref[1, :, :width] = k1_ref[0]
    o_ref[1, :, width:] = v1_ref[0]


def send_buffer(key_blocks, value_blocks, send_index):
    count = send_index.shape[0]
    _, blk, width = key_blocks.shape

    def pick(k):
        return pl.BlockSpec((1, blk, width), lambda d, t: (t[2 * d + k], 0, 0))

    grid_spec = pltpu.PrefetchScalarGridSpec(
        num_scalar_prefetch=1,
        grid=(count // 2,),
        in_specs=[pick(0), pick(1), pick(0), pick(1)],
        out_specs=pl.BlockSpec((2, blk, 2 * width), lambda d, t: (d, 0, 0)),
    )
    return pl.pallas_call(
        _send_kernel,
        grid_spec=grid_spec,
        out_shape=jax.ShapeDtypeStruct((count, blk, 2 * width), key_blocks.dtype),
        cost_estimate=pl.CostEstimate(flops=0, transcendentals=0, bytes_accessed=count * blk * width * 8),
    )(send_index, key_blocks, key_blocks, value_blocks, value_blocks)


def softmax_rows(scores):
    top = jnp.max(scores, axis=-1, keepdims=True)
    weights = jnp.exp(scores - top)
    return weights / jnp.sum(weights, axis=-1, keepdims=True)


def local(queries, keys, values, grad_out, out_weight, pattern):
    ctx_count = lax.axis_size("ctx")
    data_count = lax.axis_size("dp")
    own_index = lax.axis_index("ctx")
    rows = queries.shape[1]
    blocks = rows // BLK
    width = HEADS * DH
    scale = 1.0 / math.sqrt(DH)
    key_blocks = keys[0].reshape(blocks, BLK, width)
    value_blocks = values[0].reshape(blocks, BLK, width)
    table = pattern[0]
    owner = table // blocks
    flat_table = table.reshape(1, blocks * KSEL)
    every_table = lax.all_to_all(
        jnp.broadcast_to(flat_table, (ctx_count, blocks * KSEL)),
        "ctx",
        split_axis=0,
        concat_axis=0,
        tiled=True,
    )
    wanted = every_table // blocks == own_index
    send_index = jnp.sum(jnp.where(wanted, every_table % blocks, 0), axis=1)
    got = lax.all_to_all(
        send_buffer(key_blocks, value_blocks, send_index),
        "ctx",
        split_axis=0,
        concat_axis=0,
        tiled=True,
    )
    order = owner.reshape(-1)
    attention_flat, probs = forward_attention(queries[0], got, order)
    grad_flat = grad_out[0]
    half = out_weight.shape[1] // 2
    side = own_index % 2
    own_half = lax.dynamic_slice_in_dim(out_weight, side * half, half, axis=1)
    own_half, attention_flat = lax.optimization_barrier((own_half, attention_flat))
    mine = lax.all_to_all(
        jnp.broadcast_to(own_half[None], (data_count,) + own_half.shape),
        "dp",
        split_axis=0,
        concat_axis=0,
        tiled=True,
    ).reshape(data_count * own_half.shape[0], half)
    other = lax.ppermute(mine, "ctx", [(j, j ^ 1) for j in range(ctx_count)])
    first = jnp.where(side == 0, mine, other)
    second = jnp.where(side == 0, other, mine)
    mixed_sum = jnp.concatenate(
        [
            jnp.dot(attention_flat, first, preferred_element_type=jnp.float32),
            jnp.dot(attention_flat, second, preferred_element_type=jnp.float32),
        ],
        axis=1,
    )
    dims = (((1,), (1,)), ((), ()))
    back_sum = lax.dot_general(
        grad_flat[:, :half], first, dims, preferred_element_type=jnp.float32
    ) + lax.dot_general(grad_flat[:, half:], second, dims, preferred_element_type=jnp.float32)
    mixed = mixed_sum.astype(jnp.bfloat16)
    back = back_sum.astype(jnp.bfloat16)
    split = width // (ctx_count * data_count)
    columns = (
        attention_flat.reshape(rows, data_count, ctx_count, split)
        .transpose(0, 2, 1, 3)
        .reshape(rows, width)
    )
    partial = lax.dot_general(
        columns, grad_flat, (((0,), (0,)), ((), ())), preferred_element_type=jnp.float32
    )
    stage = lax.psum_scatter(partial, "ctx", scatter_dimension=0, tiled=True)
    query_grad = backward_attention(back, attention_flat, probs, got, order)
    stage, mixed, query_grad = lax.optimization_barrier((stage, mixed, query_grad))
    stage = stage * (1.0 / math.sqrt(rows * ctx_count * data_count))
    shard = jnp.sum(
        lax.all_to_all(
            stage.reshape(data_count, split, width), "dp", split_axis=0, concat_axis=0, tiled=True
        ),
        axis=0,
    )
    piece = shard.astype(jnp.bfloat16)
    weight_grad = lax.all_to_all(
        jnp.broadcast_to(piece[None], (ctx_count,) + piece.shape),
        "ctx",
        split_axis=0,
        concat_axis=0,
        tiled=True,
    ).reshape(ctx_count * split, width).astype(jnp.float32)
    return (mixed[None], query_grad[None], weight_grad)


def solution(mesh):
    return jax.shard_map(
        local,
        mesh=mesh,
        in_specs=(
            P("dp", "ctx", None),
            P("dp", "ctx", None),
            P("dp", "ctx", None),
            P("dp", "ctx", None),
            P("dp", None),
            P("dp", "ctx", None),
        ),
        out_specs=(P("dp", "ctx", None), P("dp", "ctx", None), P("dp", None)),
        check_vma=False,
    )
```

```python
import math

import jax
import jax.numpy as jnp
from jax import lax
from jax.experimental import pallas as pl
from jax.experimental.pallas import tpu as pltpu
from jax.sharding import PartitionSpec as P

HEADS = 16
DH = 128
BLK = 128
KSEL = 2


def _head_probs(q_ref, k0_ref, k1_ref, lanes):
    scale = 1.0 / math.sqrt(DH)
    keys = jnp.concatenate([k0_ref[0, :, lanes], k1_ref[0, :, lanes]], axis=0)
    scores = lax.dot_general(
        q_ref[:, lanes], keys, (((1,), (1,)), ((), ())), preferred_element_type=jnp.float32
    ) * scale
    top = jnp.max(scores, axis=-1, keepdims=True)
    weights = jnp.exp(scores - top)
    return weights / jnp.sum(weights, axis=-1, keepdims=True), keys


def _fwd_kernel(table, q_ref, k0_ref, k1_ref, v0_ref, v1_ref, att_ref):
    for h in range(HEADS):
        lanes = slice(h * DH, (h + 1) * DH)
        probs, _ = _head_probs(q_ref, k0_ref, k1_ref, lanes)
        vals = jnp.concatenate([v0_ref[0, :, lanes], v1_ref[0, :, lanes]], axis=0)
        att = jnp.dot(probs.astype(jnp.bfloat16), vals, preferred_element_type=jnp.float32)
        att_ref[:, lanes] = att.astype(att_ref.dtype)


def forward_attention(query_flat, got, order):
    rows, width = query_flat.shape
    blocks = rows // BLK
    heads = width // DH

    def kv(k, off):
        return pl.BlockSpec((1, BLK, width), lambda b, t: (t[KSEL * b + k], 0, off))

    grid_spec = pltpu.PrefetchScalarGridSpec(
        num_scalar_prefetch=1,
        grid=(blocks,),
        in_specs=[
            pl.BlockSpec((BLK, width), lambda b, t: (b, 0)),
            kv(0, 0),
            kv(1, 0),
            kv(0, 1),
            kv(1, 1),
        ],
        out_specs=pl.BlockSpec((BLK, width), lambda b, t: (b, 0)),
    )
    flops = blocks * heads * 4 * BLK * KSEL * BLK * DH
    return pl.pallas_call(
        _fwd_kernel,
        grid_spec=grid_spec,
        out_shape=jax.ShapeDtypeStruct((rows, width), jnp.bfloat16),
        cost_estimate=pl.CostEstimate(
            flops=flops,
            transcendentals=blocks * heads * BLK * KSEL * BLK,
            bytes_accessed=rows * width * 2 * 6,
        ),
    )(order, query_flat, got, got, got, got)


def _bwd_kernel(table, q_ref, back_ref, att_ref, k0_ref, k1_ref, v0_ref, v1_ref, out_ref):
    scale = 1.0 / math.sqrt(DH)
    for h in range(HEADS):
        lanes = slice(h * DH, (h + 1) * DH)
        probs, keys = _head_probs(q_ref, k0_ref, k1_ref, lanes)
        back = back_ref[:, lanes]
        vals = jnp.concatenate([v0_ref[0, :, lanes], v1_ref[0, :, lanes]], axis=0)
        dprobs = lax.dot_general(
            back, vals, (((1,), (1,)), ((), ())), preferred_element_type=jnp.float32
        )
        delta = jnp.sum(
            back.astype(jnp.float32) * att_ref[:, lanes].astype(jnp.float32), axis=-1, keepdims=True
        )
        dscores = (probs * (dprobs - delta)).astype(jnp.bfloat16)
        grad = jnp.dot(dscores, keys, preferred_element_type=jnp.float32) * scale
        out_ref[:, lanes] = grad.astype(out_ref.dtype)


def backward_attention(query_flat, back_flat, attention_flat, got, order):
    rows, width = back_flat.shape
    blocks = rows // BLK
    heads = width // DH

    def kv(k, off):
        return pl.BlockSpec((1, BLK, width), lambda b, t: (t[KSEL * b + k], 0, off))

    grid_spec = pltpu.PrefetchScalarGridSpec(
        num_scalar_prefetch=1,
        grid=(blocks,),
        in_specs=[
            pl.BlockSpec((BLK, width), lambda b, t: (b, 0)),
            pl.BlockSpec((BLK, width), lambda b, t: (b, 0)),
            pl.BlockSpec((BLK, width), lambda b, t: (b, 0)),
            kv(0, 0),
            kv(1, 0),
            kv(0, 1),
            kv(1, 1),
        ],
        out_specs=pl.BlockSpec((BLK, width), lambda b, t: (b, 0)),
    )
    flops = blocks * heads * 4 * BLK * KSEL * BLK * DH
    return pl.pallas_call(
        _bwd_kernel,
        grid_spec=grid_spec,
        out_shape=jax.ShapeDtypeStruct((rows, width), jnp.bfloat16),
        cost_estimate=pl.CostEstimate(
            flops=flops,
            transcendentals=blocks * heads * BLK * KSEL * BLK,
            bytes_accessed=rows * width * 2 * 8,
        ),
    )(order, query_flat, back_flat, attention_flat, got, got, got, got)


def _send_kernel(index, k0_ref, k1_ref, v0_ref, v1_ref, o_ref):
    width = k0_ref.shape[-1]
    o_ref[0, :, :width] = k0_ref[0]
    o_ref[0, :, width:] = v0_ref[0]
    o_ref[1, :, :width] = k1_ref[0]
    o_ref[1, :, width:] = v1_ref[0]


def send_buffer(key_blocks, value_blocks, send_index):
    count = send_index.shape[0]
    _, blk, width = key_blocks.shape

    def pick(k):
        return pl.BlockSpec((1, blk, width), lambda d, t: (t[2 * d + k], 0, 0))

    grid_spec = pltpu.PrefetchScalarGridSpec(
        num_scalar_prefetch=1,
        grid=(count // 2,),
        in_specs=[pick(0), pick(1), pick(0), pick(1)],
        out_specs=pl.BlockSpec((2, blk, 2 * width), lambda d, t: (d, 0, 0)),
    )
    return pl.pallas_call(
        _send_kernel,
        grid_spec=grid_spec,
        out_shape=jax.ShapeDtypeStruct((count, blk, 2 * width), key_blocks.dtype),
        cost_estimate=pl.CostEstimate(flops=0, transcendentals=0, bytes_accessed=count * blk * width * 8),
    )(send_index, key_blocks, key_blocks, value_blocks, value_blocks)


def softmax_rows(scores):
    top = jnp.max(scores, axis=-1, keepdims=True)
    weights = jnp.exp(scores - top)
    return weights / jnp.sum(weights, axis=-1, keepdims=True)


def local(queries, keys, values, grad_out, out_weight, pattern):
    ctx_count = lax.axis_size("ctx")
    data_count = lax.axis_size("dp")
    own_index = lax.axis_index("ctx")
    rows = queries.shape[1]
    blocks = rows // BLK
    width = HEADS * DH
    scale = 1.0 / math.sqrt(DH)
    key_blocks = keys[0].reshape(blocks, BLK, width)
    value_blocks = values[0].reshape(blocks, BLK, width)
    table = pattern[0]
    owner = table // blocks
    flat_table = table.reshape(1, blocks * KSEL)
    every_table = lax.all_to_all(
        jnp.broadcast_to(flat_table, (ctx_count, blocks * KSEL)),
        "ctx",
        split_axis=0,
        concat_axis=0,
        tiled=True,
    )
    wanted = every_table // blocks == own_index
    send_index = jnp.sum(jnp.where(wanted, every_table % blocks, 0), axis=1)
    got = lax.all_to_all(
        send_buffer(key_blocks, value_blocks, send_index),
        "ctx",
        split_axis=0,
        concat_axis=0,
        tiled=True,
    )
    order = owner.reshape(-1)
    attention_flat = forward_attention(queries[0], got, order)
    grad_flat = grad_out[0]
    half = out_weight.shape[1] // 2
    side = own_index % 2
    own_half = lax.dynamic_slice_in_dim(out_weight, side * half, half, axis=1)
    own_half, attention_flat = lax.optimization_barrier((own_half, attention_flat))
    mine = lax.all_to_all(
        jnp.broadcast_to(own_half[None], (data_count,) + own_half.shape),
        "dp",
        split_axis=0,
        concat_axis=0,
        tiled=True,
    ).reshape(data_count * own_half.shape[0], half)
    other = lax.ppermute(mine, "ctx", [(j, j ^ 1) for j in range(ctx_count)])
    first = jnp.where(side == 0, mine, other)
    second = jnp.where(side == 0, other, mine)
    mixed_sum = jnp.concatenate(
        [
            jnp.dot(attention_flat, first, preferred_element_type=jnp.float32),
            jnp.dot(attention_flat, second, preferred_element_type=jnp.float32),
        ],
        axis=1,
    )
    dims = (((1,), (1,)), ((), ()))
    back_sum = lax.dot_general(
        grad_flat[:, :half], first, dims, preferred_element_type=jnp.float32
    ) + lax.dot_general(grad_flat[:, half:], second, dims, preferred_element_type=jnp.float32)
    mixed = mixed_sum.astype(jnp.bfloat16)
    back = back_sum.astype(jnp.bfloat16)
    split = width // (ctx_count * data_count)
    columns = (
        attention_flat.reshape(rows, data_count, ctx_count, split)
        .transpose(0, 2, 1, 3)
        .reshape(rows, width)
    )
    partial = lax.dot_general(
        columns, grad_flat, (((0,), (0,)), ((), ())), preferred_element_type=jnp.float32
    )
    stage = lax.psum_scatter(partial, "ctx", scatter_dimension=0, tiled=True)
    query_grad = backward_attention(queries[0], back, attention_flat, got, order)
    stage, mixed, query_grad = lax.optimization_barrier((stage, mixed, query_grad))
    stage = stage * (1.0 / math.sqrt(rows * ctx_count * data_count))
    shard = jnp.sum(
        lax.all_to_all(
            stage.reshape(data_count, split, width), "dp", split_axis=0, concat_axis=0, tiled=True
        ),
        axis=0,
    )
    piece = shard.astype(jnp.bfloat16)
    weight_grad = lax.all_to_all(
        jnp.broadcast_to(piece[None], (ctx_count,) + piece.shape),
        "ctx",
        split_axis=0,
        concat_axis=0,
        tiled=True,
    ).reshape(ctx_count * split, width).astype(jnp.float32)
    return (mixed[None], query_grad[None], weight_grad)


def solution(mesh):
    return jax.shard_map(
        local,
        mesh=mesh,
        in_specs=(
            P("dp", "ctx", None),
            P("dp", "ctx", None),
            P("dp", "ctx", None),
            P("dp", "ctx", None),
            P("dp", None),
            P("dp", "ctx", None),
        ),
        out_specs=(P("dp", "ctx", None), P("dp", "ctx", None), P("dp", None)),
        check_vma=False,
    )
```

```python
import math

import jax
import jax.numpy as jnp
from jax import lax
from jax.experimental import pallas as pl
from jax.experimental.pallas import tpu as pltpu
from jax.sharding import PartitionSpec as P

HEADS = 16
DH = 128
BLK = 128
KSEL = 2


def _head_probs(q_ref, k0_ref, k1_ref, lanes):
    scale = 1.0 / math.sqrt(DH)
    keys = jnp.concatenate([k0_ref[0, :, lanes], k1_ref[0, :, lanes]], axis=0)
    scores = lax.dot_general(
        q_ref[:, lanes], keys, (((1,), (1,)), ((), ())), preferred_element_type=jnp.float32
    ) * scale
    top = jnp.max(scores, axis=-1, keepdims=True)
    weights = jnp.exp(scores - top)
    return weights / jnp.sum(weights, axis=-1, keepdims=True), keys


def _fwd_kernel(table, q_ref, k0_ref, k1_ref, v0_ref, v1_ref, att_ref):
    for h in range(HEADS):
        lanes = slice(h * DH, (h + 1) * DH)
        probs, _ = _head_probs(q_ref, k0_ref, k1_ref, lanes)
        vals = jnp.concatenate([v0_ref[0, :, lanes], v1_ref[0, :, lanes]], axis=0)
        att = jnp.dot(probs.astype(jnp.bfloat16), vals, preferred_element_type=jnp.float32)
        att_ref[:, lanes] = att.astype(att_ref.dtype)


def forward_attention(query_flat, got, order):
    rows, width = query_flat.shape
    blocks = rows // BLK
    heads = width // DH

    def kv(k, off):
        return pl.BlockSpec((1, BLK, width), lambda b, t: (t[KSEL * b + k], 0, off))

    grid_spec = pltpu.PrefetchScalarGridSpec(
        num_scalar_prefetch=1,
        grid=(blocks,),
        in_specs=[
            pl.BlockSpec((BLK, width), lambda b, t: (b, 0)),
            kv(0, 0),
            kv(1, 0),
            kv(0, 1),
            kv(1, 1),
        ],
        out_specs=pl.BlockSpec((BLK, width), lambda b, t: (b, 0)),
    )
    flops = blocks * heads * 4 * BLK * KSEL * BLK * DH
    return pl.pallas_call(
        _fwd_kernel,
        grid_spec=grid_spec,
        out_shape=jax.ShapeDtypeStruct((rows, width), jnp.bfloat16),
        cost_estimate=pl.CostEstimate(
            flops=flops,
            transcendentals=blocks * heads * BLK * KSEL * BLK,
            bytes_accessed=rows * width * 2 * 6,
        ),
    )(order, query_flat, got, got, got, got)


def _bwd_kernel(table, q_ref, back_ref, att_ref, k0_ref, k1_ref, v0_ref, v1_ref, out_ref):
    scale = 1.0 / math.sqrt(DH)
    for h in range(HEADS):
        lanes = slice(h * DH, (h + 1) * DH)
        probs, keys = _head_probs(q_ref, k0_ref, k1_ref, lanes)
        back = back_ref[:, lanes]
        vals = jnp.concatenate([v0_ref[0, :, lanes], v1_ref[0, :, lanes]], axis=0)
        dprobs = lax.dot_general(
            back, vals, (((1,), (1,)), ((), ())), preferred_element_type=jnp.float32
        )
        delta = jnp.sum(
            back.astype(jnp.float32) * att_ref[:, lanes].astype(jnp.float32), axis=-1, keepdims=True
        )
        dscores = (probs * (dprobs - delta)).astype(jnp.bfloat16)
        grad = jnp.dot(dscores, keys, preferred_element_type=jnp.float32) * scale
        out_ref[:, lanes] = grad.astype(out_ref.dtype)


def backward_attention(query_flat, back_flat, attention_flat, got, order):
    rows, width = back_flat.shape
    blocks = rows // BLK
    heads = width // DH

    def kv(k, off):
        return pl.BlockSpec((1, BLK, width), lambda b, t: (t[KSEL * b + k], 0, off))

    grid_spec = pltpu.PrefetchScalarGridSpec(
        num_scalar_prefetch=1,
        grid=(blocks,),
        in_specs=[
            pl.BlockSpec((BLK, width), lambda b, t: (b, 0)),
            pl.BlockSpec((BLK, width), lambda b, t: (b, 0)),
            pl.BlockSpec((BLK, width), lambda b, t: (b, 0)),
            kv(0, 0),
            kv(1, 0),
            kv(0, 1),
            kv(1, 1),
        ],
        out_specs=pl.BlockSpec((BLK, width), lambda b, t: (b, 0)),
    )
    flops = blocks * heads * 4 * BLK * KSEL * BLK * DH
    return pl.pallas_call(
        _bwd_kernel,
        grid_spec=grid_spec,
        out_shape=jax.ShapeDtypeStruct((rows, width), jnp.bfloat16),
        cost_estimate=pl.CostEstimate(
            flops=flops,
            transcendentals=blocks * heads * BLK * KSEL * BLK,
            bytes_accessed=rows * width * 2 * 8,
        ),
    )(order, query_flat, back_flat, attention_flat, got, got, got, got)


def _send_kernel(index, *refs):
    o_ref = refs[-1]
    slots = (len(refs) - 1) // 2
    width = refs[0].shape[-1]
    for s in range(slots):
        o_ref[s, :, :width] = refs[s][0]
        o_ref[s, :, width:] = refs[slots + s][0]


def send_buffer(key_blocks, value_blocks, send_index, slots=4):
    count = send_index.shape[0]
    _, blk, width = key_blocks.shape

    def pick(k):
        return pl.BlockSpec((1, blk, width), lambda d, t: (t[slots * d + k], 0, 0))

    grid_spec = pltpu.PrefetchScalarGridSpec(
        num_scalar_prefetch=1,
        grid=(count // slots,),
        in_specs=[pick(k) for k in range(slots)] * 2,
        out_specs=pl.BlockSpec((slots, blk, 2 * width), lambda d, t: (d, 0, 0)),
    )
    return pl.pallas_call(
        _send_kernel,
        grid_spec=grid_spec,
        out_shape=jax.ShapeDtypeStruct((count, blk, 2 * width), key_blocks.dtype),
        cost_estimate=pl.CostEstimate(flops=0, transcendentals=0, bytes_accessed=count * blk * width * 8),
    )(send_index, *([key_blocks] * slots), *([value_blocks] * slots))


def softmax_rows(scores):
    top = jnp.max(scores, axis=-1, keepdims=True)
    weights = jnp.exp(scores - top)
    return weights / jnp.sum(weights, axis=-1, keepdims=True)


def local(queries, keys, values, grad_out, out_weight, pattern):
    ctx_count = lax.axis_size("ctx")
    data_count = lax.axis_size("dp")
    own_index = lax.axis_index("ctx")
    rows = queries.shape[1]
    blocks = rows // BLK
    width = HEADS * DH
    scale = 1.0 / math.sqrt(DH)
    key_blocks = keys[0].reshape(blocks, BLK, width)
    value_blocks = values[0].reshape(blocks, BLK, width)
    table = pattern[0]
    owner = table // blocks
    flat_table = table.reshape(1, blocks * KSEL)
    every_table = lax.all_to_all(
        jnp.broadcast_to(flat_table, (ctx_count, blocks * KSEL)),
        "ctx",
        split_axis=0,
        concat_axis=0,
        tiled=True,
    )
    wanted = every_table // blocks == own_index
    send_index = jnp.sum(jnp.where(wanted, every_table % blocks, 0), axis=1)
    got = lax.all_to_all(
        send_buffer(key_blocks, value_blocks, send_index),
        "ctx",
        split_axis=0,
        concat_axis=0,
        tiled=True,
    )
    order = owner.reshape(-1)
    attention_flat = forward_attention(queries[0], got, order)
    grad_flat = grad_out[0]
    half = out_weight.shape[1] // 2
    side = own_index % 2
    own_half = lax.dynamic_slice_in_dim(out_weight, side * half, half, axis=1)
    own_half, attention_flat = lax.optimization_barrier((own_half, attention_flat))
    mine = lax.all_to_all(
        jnp.broadcast_to(own_half[None], (data_count,) + own_half.shape),
        "dp",
        split_axis=0,
        concat_axis=0,
        tiled=True,
    ).reshape(data_count * own_half.shape[0], half)
    other = lax.ppermute(mine, "ctx", [(j, j ^ 1) for j in range(ctx_count)])
    first = jnp.where(side == 0, mine, other)
    second = jnp.where(side == 0, other, mine)
    mixed_sum = jnp.concatenate(
        [
            jnp.dot(attention_flat, first, preferred_element_type=jnp.float32),
            jnp.dot(attention_flat, second, preferred_element_type=jnp.float32),
        ],
        axis=1,
    )
    dims = (((1,), (1,)), ((), ()))
    back_sum = lax.dot_general(
        grad_flat[:, :half], first, dims, preferred_element_type=jnp.float32
    ) + lax.dot_general(grad_flat[:, half:], second, dims, preferred_element_type=jnp.float32)
    mixed = mixed_sum.astype(jnp.bfloat16)
    back = back_sum.astype(jnp.bfloat16)
    split = width // (ctx_count * data_count)
    columns = (
        attention_flat.reshape(rows, data_count, ctx_count, split)
        .transpose(0, 2, 1, 3)
        .reshape(rows, width)
    )
    partial = lax.dot_general(
        columns, grad_flat, (((0,), (0,)), ((), ())), preferred_element_type=jnp.float32
    )
    stage = lax.psum_scatter(partial, "ctx", scatter_dimension=0, tiled=True)
    query_grad = backward_attention(queries[0], back, attention_flat, got, order)
    stage, mixed, query_grad = lax.optimization_barrier((stage, mixed, query_grad))
    stage = stage * (1.0 / math.sqrt(rows * ctx_count * data_count))
    shard = jnp.sum(
        lax.all_to_all(
            stage.reshape(data_count, split, width), "dp", split_axis=0, concat_axis=0, tiled=True
        ),
        axis=0,
    )
    piece = shard.astype(jnp.bfloat16)
    weight_grad = lax.all_to_all(
        jnp.broadcast_to(piece[None], (ctx_count,) + piece.shape),
        "ctx",
        split_axis=0,
        concat_axis=0,
        tiled=True,
    ).reshape(ctx_count * split, width).astype(jnp.float32)
    return (mixed[None], query_grad[None], weight_grad)


def solution(mesh):
    return jax.shard_map(
        local,
        mesh=mesh,
        in_specs=(
            P("dp", "ctx", None),
            P("dp", "ctx", None),
            P("dp", "ctx", None),
            P("dp", "ctx", None),
            P("dp", None),
            P("dp", "ctx", None),
        ),
        out_specs=(P("dp", "ctx", None), P("dp", "ctx", None), P("dp", None)),
        check_vma=False,
    )
```
